256 devices in a mesh: space: 128 (over z, y, x), sub: 2 (over core).
Axes of the slice: x: 4, y: 4, z: 8, core: 2. Of those that a mesh axis runs over, the one named last changes fastest.
Arguments:
- features: bfloat16 [262144, 128], P(('space', 'sub')), may hold values from -6 to 6
- weights: bfloat16 [27, 128, 128], replicated, may hold values from -0.125 to 0.125
- cotangent: bfloat16 [262144, 128], P(('space', 'sub')), may hold values from -6 to 6
- pair_offset: int32 [65536], P(('space', 'sub')), may hold values from 0 to 26, as said below
- pair_source: int32 [65536], P(('space', 'sub')), may hold values from 0 to 2047, as said below
- pair_target: int32 [65536], P(('space', 'sub')), may hold values from 0 to 7
- pair_rows: int32 [65536, 128], P(('space', 'sub')), may hold values from -1 to 127, as said below
- pair_count: int32 [256], P(('space', 'sub')), may hold values from 64 to 256, as said below
Outputs:
- output: bfloat16 [262144, 128], P(('space', 'sub'))
- grad_features: bfloat16 [262144, 128], P(('space', 'sub'))
- grad_weights: float32 [27, 128, 128], replicated
The draws below stay inside these ranges and needn't reach their ends.
Inputs may be any that keep to these rules, and one draw needn't show every extreme that they name: `pair_offset`: each value is a kernel offset. The input block of a pair of device d lies on device d - 1, d or d + 1 (that is, pair_source // 8 differs from d by at most one). `pair_rows`: within one pair no nonnegative row number appears twice. `pair_count`: pairs of a device at positions from its count on are not live; some device has all 256 pairs live.
All inputs are finite; a program needn't handle non-finite values.
Results may differ from the reference program's by a relative error of at most 0.001.
Values may be sent and summed in bfloat16 or wider, within the bound.
No kernel may reach another device: no remote copies, remote signals or barrier semaphores. Data moves between devices by JAX's collectives and lax.ppermute only.
A program may use at most 64 MiB of HBM per device.

```python
import math
import jax
import jax.numpy as jnp
from jax import lax

C = 128
BLK = 128
KVOL = 27
NB = 8
SHARDS = 256
PAIRS = 256
VOXELS = 262144


def draw_pair_offset(key, part):
    own_key = jax.random.fold_in(key, 11)
    values = jax.random.randint(own_key, (SHARDS * PAIRS,), 0, KVOL, dtype=jnp.int32)
    return values.at[0].set(0).at[-1].set(KVOL - 1)


def draw_pair_source(key, part):
    own_key = jax.random.fold_in(key, 12)
    key_one, key_two = jax.random.split(own_key)
    device = jnp.arange(SHARDS * PAIRS, dtype=jnp.int32) // PAIRS
    step_off = jax.random.randint(key_one, (SHARDS * PAIRS,), -1, 2, dtype=jnp.int32)
    owner_dev = jnp.clip(device + step_off, 0, SHARDS - 1)
    local_block = jax.random.randint(key_two, (SHARDS * PAIRS,), 0, NB, dtype=jnp.int32)
    values = owner_dev * NB + local_block
    return values.at[0].set(0).at[-1].set(SHARDS * NB - 1)


def draw_pair_target(key, part):
    own_key = jax.random.fold_in(key, 13)
    values = jax.random.randint(own_key, (SHARDS * PAIRS,), 0, NB, dtype=jnp.int32)
    return values.at[0].set(0).at[-1].set(NB - 1)


def draw_pair_rows(key, part):
    own_key = jax.random.fold_in(key, 14)
    key_one, key_two = jax.random.split(own_key)
    row_shift = jax.random.randint(key_one, (SHARDS * PAIRS, 1), 0, BLK, dtype=jnp.int32)
    keep_row = jax.random.randint(key_two, (SHARDS * PAIRS, BLK), 0, 10, dtype=jnp.int32) < 7
    columns = jnp.arange(BLK, dtype=jnp.int32)
    values = jnp.where(keep_row, (columns[None, :] + row_shift) % BLK, -1)
    first_row = jnp.where(columns > 0, columns, -1)
    return values.at[0].set(first_row).astype(jnp.int32)


def draw_pair_count(key, part):
    own_key = jax.random.fold_in(key, 15)
    key_one, key_two = jax.random.split(own_key)
    values = jax.random.randint(key_one, (SHARDS,), PAIRS // 4, 3 * PAIRS // 4 + 1, dtype=jnp.int32)
    full_dev = jax.random.randint(key_two, (), 0, SHARDS, dtype=jnp.int32)
    return jnp.where(jnp.arange(SHARDS, dtype=jnp.int32) == full_dev, PAIRS, values).astype(jnp.int32)


def levels(stream_key, shape, shards, least, high):
    level, own = 1.0, jax.random.fold_in(stream_key, 6)
    for dim, parts in shards:
        steps = jnp.exp(jax.random.uniform(jax.random.fold_in(own, dim), (parts,), jnp.float32, least / len(shards), high / len(shards)))
        level = level * jnp.repeat(steps, shape[dim] // parts).reshape([-1 if axis == dim else 1 for axis in range(len(shape))])
    return level


def centred(key, dims, scale, reach, cuts=(), kind=jnp.bfloat16):
    result = scale * jax.random.normal(key, dims, jnp.float32)
    if cuts:
        result = result * levels(key, dims, cuts, -0.22, 0.18)
    return jnp.clip(result, -reach, reach).astype(kind)


def setup_inputs(seed: int = 0) -> dict:
    keys = jax.random.split(jax.random.key(seed), 9)
    features = centred(keys[0], (VOXELS, C), 1.0, 6.0, ((0, 256),))
    weights = centred(keys[1], (KVOL, C, C), (16 * C) ** -0.5, 0.125)
    cotangent = centred(keys[2], (VOXELS, C), 1.0, 6.0, ((0, 256),))
    pair_offset = draw_pair_offset(jax.random.fold_in(keys[8], 71), 0)
    pair_source = draw_pair_source(jax.random.fold_in(keys[8], 71), 0)
    pair_target = draw_pair_target(jax.random.fold_in(keys[8], 71), 0)
    pair_rows = draw_pair_rows(jax.random.fold_in(keys[8], 71), 0)
    pair_count = draw_pair_count(jax.random.fold_in(keys[8], 71), 0)
    return {"features": features, "weights": weights, "cotangent": cotangent, "pair_offset": pair_offset, "pair_source": pair_source, "pair_target": pair_target, "pair_rows": pair_rows, "pair_count": pair_count}


def reference(features, weights, cotangent, pair_offset, pair_source, pair_target, pair_rows, pair_count):
    channels = features.shape[1]
    blocks_all = SHARDS * NB
    cot_blocks = cotangent.reshape(blocks_all, BLK, channels)
    weight_wide = weights.astype(jnp.float32)
    positions = jnp.arange(PAIRS, dtype=jnp.int32)
    pieces = (pair_offset.reshape(SHARDS, PAIRS), pair_source.reshape(SHARDS, PAIRS), pair_target.reshape(SHARDS, PAIRS), pair_rows.reshape(SHARDS, PAIRS, BLK), pair_count, jnp.arange(SHARDS, dtype=jnp.int32))

    def advance(state_in, item_now):
        out_sum, returned_sum, grad_sum = state_in
        g_off, g_source, g_target, row_map, live_count, device = item_now
        usable = (row_map >= 0) & (positions < live_count)[:, None]
        row_index = (g_source[:, None] * BLK + jnp.maximum(row_map, 0)).astype(jnp.int32)
        gathered = jnp.where(usable[..., None], features[row_index].astype(jnp.float32), jnp.float32(0.0))
        chosen = weight_wide[g_off]
        target_block = (device * NB + g_target).astype(jnp.int32)
        grad_out = cot_blocks[target_block].astype(jnp.float32)
        product = jnp.einsum('gbc,gcd->gbd', gathered, chosen, precision=lax.Precision.HIGHEST)
        out_sum = out_sum.at[target_block].add(product)
        returned = jnp.einsum('gbd,gcd->gbc', grad_out, chosen, precision=lax.Precision.HIGHEST)
        returned = jnp.where(usable[..., None], returned, jnp.float32(0.0))
        returned_sum = returned_sum.at[row_index.reshape(-1)].add(returned.reshape(-1, channels))
        pair_grad = jnp.einsum('gbc,gbd->gcd', gathered, grad_out, precision=lax.Precision.HIGHEST)
        grad_sum = grad_sum.at[g_off].add(pair_grad)
        return ((out_sum, returned_sum, grad_sum), None)
    start = (jnp.zeros((blocks_all, BLK, channels), jnp.float32), jnp.zeros((blocks_all * BLK, channels), jnp.float32), jnp.zeros((KVOL, channels, channels), jnp.float32))
    (out_sum, returned_sum, grad_sum), _ = lax.scan(advance, start, pieces)
    output = out_sum.reshape(blocks_all * BLK, channels).astype(jnp.bfloat16)
    grad_features = returned_sum.astype(jnp.bfloat16)
    grad_weights = grad_sum * (1.0 / math.sqrt(VOXELS))
    return (output, grad_features, grad_weights)
```

```python
import math

import jax
import jax.numpy as jnp
from jax import lax
from jax.sharding import PartitionSpec as P

BLK = 128


def passed_along(value, axis, steps):
    count = lax.axis_size(axis)
    leading, last = (max(0, -steps), min(count, count - steps))
    return lax.ppermute(value, axis, [(source, source + steps) for source in range(leading, last)])


def summed_everywhere(value, axis):
    count = lax.axis_size(axis)
    if count & (count - 1) or value.size % count:
        return lax.psum(value, axis)
    me = lax.axis_index(axis)
    flat = value.reshape(-1)
    masks = [1 << step for step in range(count.bit_length() - 1)]
    for mask in masks:
        half = flat.shape[0] // 2
        upper = (me & mask) != 0
        send = jnp.where(upper, flat[:half], flat[half:])
        keep = jnp.where(upper, flat[half:], flat[:half])
        flat = keep + lax.ppermute(send, axis, [(i, i ^ mask) for i in range(count)])
    for mask in reversed(masks):
        upper = (me & mask) != 0
        other = lax.ppermute(flat, axis, [(i, i ^ mask) for i in range(count)])
        flat = jnp.where(upper, jnp.concatenate([other, flat]), jnp.concatenate([flat, other]))
    return flat.reshape(value.shape)


def grouped(array_in, group_size):
    return array_in.reshape((array_in.shape[0] // group_size, group_size) + array_in.shape[1:])


def picker(index, count, dtype):
    return (index[:, None] == jnp.arange(count, dtype=jnp.int32)[None, :]).astype(dtype)


def permuter(row_map, usable, dtype):
    columns = jnp.arange(row_map.shape[1], dtype=jnp.int32)
    return ((row_map[..., None] == columns[None, None, :]) & usable[..., None]).astype(dtype)


def forward_sweep(window, weights, grad_blocks, rulebook, myself, blocks):
    g_off_all, source_all, target_all, row_map_all, live_count = rulebook
    channels = window.shape[1]
    kernel_count = weights.shape[0]
    window_blocks = window.reshape(3 * blocks, BLK, channels)
    group_size = 16
    positions = jnp.arange(g_off_all.shape[0], dtype=jnp.int32)
    relative = source_all // blocks - myself
    window_block = (relative + 1) * blocks + source_all % blocks
    pieces = (
        grouped(g_off_all, group_size),
        grouped(window_block, group_size),
        grouped(target_all, group_size),
        grouped(row_map_all, group_size),
        grouped(positions, group_size),
    )
    highest = lax.Precision.HIGHEST

    def advance(state_in, item_now):
        out_sum, returned_sum, grad_sum = state_in
        g_off, g_block, g_target, row_map, g_pos = item_now
        usable = (row_map >= 0) & (g_pos < live_count[0])[:, None]
        perm = permuter(row_map, usable, jnp.bfloat16)
        block_pick = picker(g_block, 3 * blocks, jnp.bfloat16)
        rows_in = jnp.einsum(
            "gk,kbc->gbc", block_pick, window_blocks, preferred_element_type=jnp.float32
        ).astype(jnp.bfloat16)
        gathered = jnp.einsum(
            "grs,gsc->grc", perm, rows_in, preferred_element_type=jnp.float32
        ).astype(jnp.bfloat16)
        off_pick = picker(g_off, kernel_count, jnp.bfloat16)
        chosen = jnp.einsum(
            "gk,kcd->gcd", off_pick, weights, preferred_element_type=jnp.float32
        ).astype(jnp.bfloat16)
        product = jnp.einsum("gbc,gcd->gbd", gathered, chosen, preferred_element_type=jnp.float32)
        target_pick = picker(g_target, blocks, jnp.float32)
        out_sum = out_sum + jnp.einsum("gt,gbd->tbd", target_pick, product, precision=highest)
        grad_out = jnp.einsum(
            "gt,tbd->gbd",
            target_pick.astype(jnp.bfloat16),
            grad_blocks,
            preferred_element_type=jnp.float32,
        ).astype(jnp.bfloat16)
        pair_grad = jnp.einsum(
            "gbc,gbd->gcd", gathered, grad_out, preferred_element_type=jnp.float32
        )
        grad_sum = grad_sum + jnp.einsum(
            "gk,gcd->kcd", off_pick.astype(jnp.float32), pair_grad, precision=highest
        )
        moved = jnp.einsum(
            "grs,grd->gsd", perm, grad_out, preferred_element_type=jnp.float32
        ).astype(jnp.bfloat16)
        returned = jnp.einsum("gsd,gcd->gsc", moved, chosen, preferred_element_type=jnp.float32)
        returned_sum = returned_sum + jnp.einsum(
            "gk,gsc->ksc", block_pick.astype(jnp.float32), returned, precision=highest
        )
        return ((out_sum, returned_sum, grad_sum), None)

    back_blocks = 3 * blocks
    start = (
        jnp.zeros((blocks, BLK, channels), jnp.float32),
        jnp.zeros((back_blocks, BLK, channels), jnp.float32),
        jnp.zeros((kernel_count, channels, channels), jnp.float32),
    )
    (out_sum, returned_sum, grad_sum), _ = lax.scan(advance, start, pieces)
    return (out_sum, returned_sum, grad_sum)


def on_device(
    features, weights, cotangent, pair_offset, pair_source, pair_target, pair_rows, pair_count
):
    axis_count = lax.axis_size(("space", "sub"))
    myself = lax.axis_index(("space", "sub"))
    local_rows = features.shape[0]
    blocks = local_rows // BLK
    channels = features.shape[1]
    before = passed_along(features, ("space", "sub"), 1)
    next_side = passed_along(features, ("space", "sub"), -1)
    window = jnp.concatenate([before, features, next_side], axis=0)
    grad_blocks = cotangent.reshape(blocks, BLK, channels)
    rulebook = (pair_offset, pair_source, pair_target, pair_rows, pair_count)
    out_sum, returned_sum, grad_sum = forward_sweep(
        window, weights, grad_blocks, rulebook, myself, blocks
    )
    low_part = returned_sum[:blocks].reshape(local_rows, channels)
    middle = returned_sum[blocks : 2 * blocks].reshape(local_rows, channels)
    high_part = returned_sum[2 * blocks :].reshape(local_rows, channels)
    from_next = passed_along(low_part, ("space", "sub"), -1)
    from_prev = passed_along(high_part, ("space", "sub"), 1)
    grad_features = (middle + from_next + from_prev).astype(jnp.bfloat16)
    output = out_sum.reshape(local_rows, channels).astype(jnp.bfloat16)
    grad_sum = grad_sum * (1.0 / math.sqrt(axis_count * local_rows))
    grand_total = summed_everywhere(grad_sum, ("space", "sub"))
    return (output, grad_features, grand_total)


def solution(mesh):
    placed = (
        P(("space", "sub"), None),
        P(),
        P(("space", "sub"), None),
        P(("space", "sub")),
        P(("space", "sub")),
        P(("space", "sub")),
        P(("space", "sub"), None),
        P(("space", "sub")),
    )
    return jax.shard_map(
        on_device,
        mesh=mesh,
        in_specs=placed,
        out_specs=(P(("space", "sub"), None), P(("space", "sub"), None), P()),
        check_vma=False,
    )
```

```python
import math

import jax
import jax.numpy as jnp
from jax import lax
from jax.experimental import pallas as pl
from jax.experimental.pallas import tpu as pltpu
from jax.sharding import PartitionSpec as P

BLK = 128


def passed_along(value, axis, steps):
    count = lax.axis_size(axis)
    leading, last = (max(0, -steps), min(count, count - steps))
    return lax.ppermute(value, axis, [(source, source + steps) for source in range(leading, last)])


def summed_everywhere(value, axis):
    count = lax.axis_size(axis)
    if count & (count - 1) or value.size % count:
        return lax.psum(value, axis)
    me = lax.axis_index(axis)
    flat = value.reshape(-1)
    masks = [1 << step for step in range(count.bit_length() - 1)]
    for mask in masks:
        half = flat.shape[0] // 2
        upper = (me & mask) != 0
        send = jnp.where(upper, flat[:half], flat[half:])
        keep = jnp.where(upper, flat[half:], flat[:half])
        flat = keep + lax.ppermute(send, axis, [(i, i ^ mask) for i in range(count)])
    for mask in reversed(masks):
        upper = (me & mask) != 0
        other = lax.ppermute(flat, axis, [(i, i ^ mask) for i in range(count)])
        flat = jnp.where(upper, jnp.concatenate([other, flat]), jnp.concatenate([flat, other]))
    return flat.reshape(value.shape)


def grouped(array_in, group_size):
    return array_in.reshape((array_in.shape[0] // group_size, group_size) + array_in.shape[1:])


def picker(index, count, dtype):
    return (index[:, None] == jnp.arange(count, dtype=jnp.int32)[None, :]).astype(dtype)


def permuter(row_map, usable, dtype):
    columns = jnp.arange(row_map.shape[1], dtype=jnp.int32)
    return ((row_map[..., None] == columns[None, None, :]) & usable[..., None]).astype(dtype)


def sweep_kernel(offsets, blocks_at, targets, live, window_ref, weights_ref, cot_ref, rows_ref,
                 out_ref, ret_ref, grad_ref):
    out_ref[...] = jnp.zeros(out_ref.shape, out_ref.dtype)
    ret_ref[...] = jnp.zeros(ret_ref.shape, ret_ref.dtype)
    grad_ref[...] = jnp.zeros(grad_ref.shape, grad_ref.dtype)
    source_rows = lax.broadcasted_iota(jnp.int32, (BLK, BLK), 0)
    lhs_rows = (((0,), (0,)), ((), ()))
    rhs_rows = (((1,), (1,)), ((), ()))

    def advance(p, carry):
        kernel_at = offsets[p]
        block_at = blocks_at[p]
        target_at = targets[p]
        picks = (rows_ref[p] == source_rows).astype(jnp.bfloat16)
        chosen = weights_ref[kernel_at]
        grad_out = cot_ref[target_at]
        gathered = lax.dot_general(
            picks, window_ref[block_at], lhs_rows, preferred_element_type=jnp.float32
        ).astype(jnp.bfloat16)
        moved = jnp.dot(picks, grad_out, preferred_element_type=jnp.float32).astype(jnp.bfloat16)
        out_ref[target_at] += jnp.dot(gathered, chosen, preferred_element_type=jnp.float32)
        ret_ref[block_at] += lax.dot_general(
            moved, chosen, rhs_rows, preferred_element_type=jnp.float32
        )
        grad_ref[kernel_at] += lax.dot_general(
            gathered, grad_out, lhs_rows, preferred_element_type=jnp.float32
        )
        return carry

    lax.fori_loop(0, live[0], advance, 0)


def forward_sweep(window, weights, grad_blocks, rulebook, myself, blocks):
    g_off_all, source_all, target_all, row_map_all, live_count = rulebook
    channels = window.shape[1]
    kernel_count = weights.shape[0]
    pair_slots = g_off_all.shape[0]
    window_blocks = window.reshape(3 * blocks, BLK, channels)
    relative = source_all // blocks - myself
    window_block = jnp.clip((relative + 1) * blocks + source_all % blocks, 0, 3 * blocks - 1)
    offsets = jnp.clip(g_off_all, 0, kernel_count - 1)
    targets = jnp.clip(target_all, 0, blocks - 1)
    live = jnp.clip(live_count, 0, pair_slots)
    smem = pl.BlockSpec(memory_space=pltpu.SMEM)
    vmem = pl.BlockSpec(memory_space=pltpu.VMEM)
    return pl.pallas_call(
        sweep_kernel,
        out_shape=(
            jax.ShapeDtypeStruct((blocks, BLK, channels), jnp.float32),
            jax.ShapeDtypeStruct((3 * blocks, BLK, channels), jnp.float32),
            jax.ShapeDtypeStruct((kernel_count, channels, channels), jnp.float32),
        ),
        in_specs=[smem, smem, smem, smem, vmem, vmem, vmem, vmem],
        out_specs=(vmem, vmem, vmem),
    )(offsets, window_block, targets, live, window_blocks, weights, grad_blocks,
      row_map_all.reshape(pair_slots, 1, BLK))


def on_device(
    features, weights, cotangent, pair_offset, pair_source, pair_target, pair_rows, pair_count
):
    axis_count = lax.axis_size(("space", "sub"))
    myself = lax.axis_index(("space", "sub"))
    local_rows = features.shape[0]
    blocks = local_rows // BLK
    channels = features.shape[1]
    before = passed_along(features, ("space", "sub"), 1)
    next_side = passed_along(features, ("space", "sub"), -1)
    window = jnp.concatenate([before, features, next_side], axis=0)
    grad_blocks = cotangent.reshape(blocks, BLK, channels)
    rulebook = (pair_offset, pair_source, pair_target, pair_rows, pair_count)
    out_sum, returned_sum, grad_sum = forward_sweep(
        window, weights, grad_blocks, rulebook, myself, blocks
    )
    low_part = returned_sum[:blocks].reshape(local_rows, channels)
    middle = returned_sum[blocks : 2 * blocks].reshape(local_rows, channels)
    high_part = returned_sum[2 * blocks :].reshape(local_rows, channels)
    from_next = passed_along(low_part, ("space", "sub"), -1)
    from_prev = passed_along(high_part, ("space", "sub"), 1)
    grad_features = (middle + from_next + from_prev).astype(jnp.bfloat16)
    output = out_sum.reshape(local_rows, channels).astype(jnp.bfloat16)
    grad_sum = grad_sum * (1.0 / math.sqrt(axis_count * local_rows))
    grand_total = summed_everywhere(grad_sum, ("space", "sub"))
    return (output, grad_features, grand_total)


def solution(mesh):
    placed = (
        P(("space", "sub"), None),
        P(),
        P(("space", "sub"), None),
        P(("space", "sub")),
        P(("space", "sub")),
        P(("space", "sub")),
        P(("space", "sub"), None),
        P(("space", "sub")),
    )
    return jax.shard_map(
        on_device,
        mesh=mesh,
        in_specs=placed,
        out_specs=(P(("space", "sub"), None), P(("space", "sub"), None), P()),
        check_vma=False,
    )
```

```python
import math

import jax
import jax.numpy as jnp
from jax import lax
from jax.experimental import pallas as pl
from jax.experimental.pallas import tpu as pltpu
from jax.sharding import PartitionSpec as P

BLK = 128


def passed_along(value, axis, steps):
    count = lax.axis_size(axis)
    leading, last = (max(0, -steps), min(count, count - steps))
    return lax.ppermute(value, axis, [(source, source + steps) for source in range(leading, last)])


def summed_everywhere(value, axis):
    count = lax.axis_size(axis)
    if count & (count - 1) or value.size % count:
        return lax.psum(value, axis)
    me = lax.axis_index(axis)
    flat = value.reshape(-1)
    masks = [1 << step for step in range(count.bit_length() - 1)]
    for mask in masks:
        half = flat.shape[0] // 2
        upper = (me & mask) != 0
        send = jnp.where(upper, flat[:half], flat[half:])
        keep = jnp.where(upper, flat[half:], flat[:half])
        flat = keep + lax.ppermute(send, axis, [(i, i ^ mask) for i in range(count)])
    for mask in reversed(masks):
        upper = (me & mask) != 0
        other = lax.ppermute(flat, axis, [(i, i ^ mask) for i in range(count)])
        flat = jnp.where(upper, jnp.concatenate([other, flat]), jnp.concatenate([flat, other]))
    return flat.reshape(value.shape)


def grouped(array_in, group_size):
    return array_in.reshape((array_in.shape[0] // group_size, group_size) + array_in.shape[1:])


def picker(index, count, dtype):
    return (index[:, None] == jnp.arange(count, dtype=jnp.int32)[None, :]).astype(dtype)


def permuter(row_map, usable, dtype):
    columns = jnp.arange(row_map.shape[1], dtype=jnp.int32)
    return ((row_map[..., None] == columns[None, None, :]) & usable[..., None]).astype(dtype)


def sweep_kernel(offsets, blocks_at, targets, live, window_ref, weights_ref, weights_t_ref, cot_ref,
                 rows_ref, out_ref, ret_ref, grad_ref):
    out_ref[...] = jnp.zeros(out_ref.shape, out_ref.dtype)
    ret_ref[...] = jnp.zeros(ret_ref.shape, ret_ref.dtype)
    grad_ref[...] = jnp.zeros(grad_ref.shape, grad_ref.dtype)
    source_rows = lax.broadcasted_iota(jnp.int32, (BLK, BLK), 0)

    def advance(p, carry):
        kernel_at = offsets[p]
        block_at = blocks_at[p]
        target_at = targets[p]
        picks = ((rows_ref[p] == source_rows) & (p < live[0])).astype(jnp.bfloat16)
        grad_out = cot_ref[target_at]
        gathered_t = jnp.dot(
            window_ref[block_at], picks, preferred_element_type=jnp.float32
        ).astype(jnp.bfloat16)
        moved = jnp.dot(picks, grad_out, preferred_element_type=jnp.float32).astype(jnp.bfloat16)
        out_ref[target_at] += jnp.dot(
            weights_t_ref[kernel_at], gathered_t, preferred_element_type=jnp.float32
        )
        ret_ref[block_at] += jnp.dot(
            moved, weights_t_ref[kernel_at], preferred_element_type=jnp.float32
        )
        grad_ref[kernel_at] += jnp.dot(gathered_t, grad_out, preferred_element_type=jnp.float32)
        return carry

    lax.fori_loop(0, rows_ref.shape[0], advance, 0, unroll=UNROLL)


UNROLL = 4


def forward_sweep(window, weights, grad_blocks, rulebook, myself, blocks):
    g_off_all, source_all, target_all, row_map_all, live_count = rulebook
    channels = window.shape[1]
    kernel_count = weights.shape[0]
    pair_slots = g_off_all.shape[0]
    window_t = window.reshape(3 * blocks, BLK, channels).transpose(0, 2, 1)
    weights_t = weights.transpose(0, 2, 1)
    relative = source_all // blocks - myself
    window_block = jnp.clip((relative + 1) * blocks + source_all % blocks, 0, 3 * blocks - 1)
    offsets = jnp.clip(g_off_all, 0, kernel_count - 1)
    targets = jnp.clip(target_all, 0, blocks - 1)
    live = jnp.clip(live_count, 0, pair_slots)
    smem = pl.BlockSpec(memory_space=pltpu.SMEM)
    vmem = pl.BlockSpec(memory_space=pltpu.VMEM)
    out_t, returned, grad = pl.pallas_call(
        sweep_kernel,
        out_shape=(
            jax.ShapeDtypeStruct((blocks, channels, BLK), jnp.float32),
            jax.ShapeDtypeStruct((3 * blocks, BLK, channels), jnp.float32),
            jax.ShapeDtypeStruct((kernel_count, channels, channels), jnp.float32),
        ),
        in_specs=[smem, smem, smem, smem, vmem, vmem, vmem, vmem, vmem],
        out_specs=(vmem, vmem, vmem),
    )(offsets, window_block, targets, live, window_t, weights, weights_t, grad_blocks,
      row_map_all.reshape(pair_slots, 1, BLK))
    return out_t.transpose(0, 2, 1), returned, grad


def on_device(
    features, weights, cotangent, pair_offset, pair_source, pair_target, pair_rows, pair_count
):
    axis_count = lax.axis_size(("space", "sub"))
    myself = lax.axis_index(("space", "sub"))
    local_rows = features.shape[0]
    blocks = local_rows // BLK
    channels = features.shape[1]
    before = passed_along(features, ("space", "sub"), 1)
    next_side = passed_along(features, ("space", "sub"), -1)
    window = jnp.concatenate([before, features, next_side], axis=0)
    grad_blocks = cotangent.reshape(blocks, BLK, channels)
    rulebook = (pair_offset, pair_source, pair_target, pair_rows, pair_count)
    out_sum, returned_sum, grad_sum = forward_sweep(
        window, weights, grad_blocks, rulebook, myself, blocks
    )
    low_part = returned_sum[:blocks].reshape(local_rows, channels)
    middle = returned_sum[blocks : 2 * blocks].reshape(local_rows, channels)
    high_part = returned_sum[2 * blocks :].reshape(local_rows, channels)
    from_next = passed_along(low_part, ("space", "sub"), -1)
    from_prev = passed_along(high_part, ("space", "sub"), 1)
    grad_features = (middle + from_next + from_prev).astype(jnp.bfloat16)
    output = out_sum.reshape(local_rows, channels).astype(jnp.bfloat16)
    grad_sum = grad_sum * (1.0 / math.sqrt(axis_count * local_rows))
    grand_total = summed_everywhere(grad_sum, ("space", "sub"))
    return (output, grad_features, grand_total)


def solution(mesh):
    placed = (
        P(("space", "sub"), None),
        P(),
        P(("space", "sub"), None),
        P(("space", "sub")),
        P(("space", "sub")),
        P(("space", "sub")),
        P(("space", "sub"), None),
        P(("space", "sub")),
    )
    return jax.shard_map(
        on_device,
        mesh=mesh,
        in_specs=placed,
        out_specs=(P(("space", "sub"), None), P(("space", "sub"), None), P()),
        check_vma=False,
    )
```

```python
import functools
import math

import jax
import jax.numpy as jnp
from jax import lax
from jax.experimental import pallas as pl
from jax.experimental.pallas import tpu as pltpu
from jax.sharding import PartitionSpec as P

BLK = 128


def passed_along(value, axis, steps):
    count = lax.axis_size(axis)
    leading, last = (max(0, -steps), min(count, count - steps))
    return lax.ppermute(value, axis, [(source, source + steps) for source in range(leading, last)])


def summed_everywhere(value, axis, work, state):
    count = lax.axis_size(axis)
    me = lax.axis_index(axis)
    flat = value.reshape(-1)
    masks = [1 << step for step in range(count.bit_length() - 1)]
    step = 0
    for mask in masks:
        half = flat.shape[0] // 2
        upper = (me & mask) != 0
        send = jnp.where(upper, flat[:half], flat[half:])
        keep = jnp.where(upper, flat[half:], flat[:half])
        received = lax.ppermute(send, axis, [(i, i ^ mask) for i in range(count)])
        state = work(step, state)
        flat, state = lax.optimization_barrier((keep + received, state))
        step += 1
    for mask in reversed(masks):
        upper = (me & mask) != 0
        other = lax.ppermute(flat, axis, [(i, i ^ mask) for i in range(count)])
        state = work(step, state)
        flat = jnp.where(upper, jnp.concatenate([other, flat]), jnp.concatenate([flat, other]))
        flat, state = lax.optimization_barrier((flat, state))
        step += 1
    return flat.reshape(value.shape), state


def grouped(array_in, group_size):
    return array_in.reshape((array_in.shape[0] // group_size, group_size) + array_in.shape[1:])


def picker(index, count, dtype):
    return (index[:, None] == jnp.arange(count, dtype=jnp.int32)[None, :]).astype(dtype)


def permuter(row_map, usable, dtype):
    columns = jnp.arange(row_map.shape[1], dtype=jnp.int32)
    return ((row_map[..., None] == columns[None, None, :]) & usable[..., None]).astype(dtype)


def grad_kernel(offsets, blocks_at, targets, live, window_ref, cot_ref, rows_ref, grad_ref,
                gathered_ref):
    grad_ref[...] = jnp.zeros(grad_ref.shape, grad_ref.dtype)
    source_rows = lax.broadcasted_iota(jnp.int32, (BLK, BLK), 0)

    def advance(p, carry):
        kernel_at = offsets[p]
        picks = ((rows_ref[p] == source_rows) & (p < live[0])).astype(jnp.bfloat16)
        gathered_t = jnp.dot(
            window_ref[blocks_at[p]], picks, preferred_element_type=jnp.float32
        ).astype(jnp.bfloat16)
        gathered_ref[p] = gathered_t
        grad_ref[kernel_at] += jnp.dot(
            gathered_t, cot_ref[targets[p]], preferred_element_type=jnp.float32
        )
        return carry

    lax.fori_loop(0, rows_ref.shape[0], advance, 0, unroll=UNROLL)


def sweep_kernel(first, offsets, blocks_at, targets, live, weights_t_ref, cot_ref, rows_ref,
                 gathered_ref, out_in, ret_in, out_ref, ret_ref):
    out_ref[...] = out_in[...]
    ret_ref[...] = ret_in[...]
    source_rows = lax.broadcasted_iota(jnp.int32, (BLK, BLK), 0)

    def advance(p, carry):
        pair = first + p
        kernel_at = offsets[pair]
        target_at = targets[pair]
        picks = ((rows_ref[p] == source_rows) & (pair < live[0])).astype(jnp.bfloat16)
        moved = jnp.dot(
            picks, cot_ref[target_at], preferred_element_type=jnp.float32
        ).astype(jnp.bfloat16)
        out_ref[target_at] += jnp.dot(
            weights_t_ref[kernel_at], gathered_ref[p], preferred_element_type=jnp.float32
        )
        ret_ref[blocks_at[pair]] += jnp.dot(
            moved, weights_t_ref[kernel_at], preferred_element_type=jnp.float32
        )
        return carry

    lax.fori_loop(0, rows_ref.shape[0], advance, 0, unroll=UNROLL)


UNROLL = 4
CHUNKS = 8
FIRST_STEP = 1


def rulebook_scalars(rulebook, myself, blocks, kernel_count):
    g_off_all, source_all, target_all, row_map_all, live_count = rulebook
    pair_slots = g_off_all.shape[0]
    relative = source_all // blocks - myself
    window_block = jnp.clip((relative + 1) * blocks + source_all % blocks, 0, 3 * blocks - 1)
    offsets = jnp.clip(g_off_all, 0, kernel_count - 1)
    targets = jnp.clip(target_all, 0, blocks - 1)
    live = jnp.clip(live_count, 0, pair_slots)
    return offsets, window_block, targets, live, row_map_all.reshape(pair_slots, 1, BLK)


def grad_sweep(window, grad_blocks, scalars, kernel_count):
    channels = window.shape[1]
    rows = scalars[-1]
    window_t = window.reshape(-1, BLK, channels).transpose(0, 2, 1)
    smem = pl.BlockSpec(memory_space=pltpu.SMEM)
    vmem = pl.BlockSpec(memory_space=pltpu.VMEM)
    return pl.pallas_call(
        grad_kernel,
        out_shape=(
            jax.ShapeDtypeStruct((kernel_count, channels, channels), jnp.float32),
            jax.ShapeDtypeStruct((rows.shape[0], channels, BLK), jnp.bfloat16),
        ),
        in_specs=[smem, smem, smem, smem, vmem, vmem, vmem],
        out_specs=(vmem, vmem),
    )(*scalars[:4], window_t, grad_blocks, rows)


def forward_chunk(weights_t, grad_blocks, scalars, gathered, sums, chunk, chunk_size):
    out_sum, returned_sum = sums
    smem = pl.BlockSpec(memory_space=pltpu.SMEM)

    def whole(array):
        return pl.BlockSpec(array.shape, lambda i: (0,) * array.ndim)

    def part(array):
        return pl.BlockSpec((chunk_size,) + array.shape[1:], lambda i: (chunk,) + (0,) * (array.ndim - 1))

    rows = scalars[4]
    return pl.pallas_call(
        functools.partial(sweep_kernel, chunk * chunk_size),
        grid=(1,),
        out_shape=(
            jax.ShapeDtypeStruct(out_sum.shape, jnp.float32),
            jax.ShapeDtypeStruct(returned_sum.shape, jnp.float32),
        ),
        in_specs=[smem, smem, smem, smem, whole(weights_t), whole(grad_blocks), part(rows),
                  part(gathered), whole(out_sum), whole(returned_sum)],
        out_specs=(whole(out_sum), whole(returned_sum)),
        input_output_aliases={8: 0, 9: 1},
    )(*scalars[:4], weights_t, grad_blocks, rows, gathered, out_sum, returned_sum)


def on_device(
    features, weights, cotangent, pair_offset, pair_source, pair_target, pair_rows, pair_count
):
    axis_count = lax.axis_size(("space", "sub"))
    myself = lax.axis_index(("space", "sub"))
    local_rows = features.shape[0]
    blocks = local_rows // BLK
    channels = features.shape[1]
    before = passed_along(features, ("space", "sub"), 1)
    next_side = passed_along(features, ("space", "sub"), -1)
    window = jnp.concatenate([before, features, next_side], axis=0)
    grad_blocks = cotangent.reshape(blocks, BLK, channels)
    rulebook = (pair_offset, pair_source, pair_target, pair_rows, pair_count)
    kernel_count = weights.shape[0]
    scalars = rulebook_scalars(rulebook, myself, blocks, kernel_count)
    grad_sum, gathered = grad_sweep(window, grad_blocks, scalars, kernel_count)
    grad_sum = grad_sum * (1.0 / math.sqrt(axis_count * local_rows))
    weights_t = weights.transpose(0, 2, 1)
    pair_slots = pair_offset.shape[0]
    chunk_count = CHUNKS if pair_slots % CHUNKS == 0 else 1
    chunk_size = pair_slots // chunk_count
    first_step = FIRST_STEP if axis_count & (axis_count - 1) == 0 else 0

    def work(step, sums):
        chunk = step - first_step
        if 0 <= chunk < chunk_count:
            return forward_chunk(weights_t, grad_blocks, scalars, gathered, sums, chunk, chunk_size)
        return sums

    sums = (
        jnp.zeros((blocks, channels, BLK), jnp.float32),
        jnp.zeros((3 * blocks, BLK, channels), jnp.float32),
    )
    if axis_count & (axis_count - 1) or grad_sum.size % axis_count:
        grand_total = lax.psum(grad_sum, ("space", "sub"))
        for chunk in range(chunk_count):
            sums = work(chunk + first_step, sums)
    else:
        grand_total, sums = summed_everywhere(grad_sum, ("space", "sub"), work, sums)
    out_t, returned_sum = sums
    out_sum = out_t.transpose(0, 2, 1)
    low_part = returned_sum[:blocks].reshape(local_rows, channels)
    middle = returned_sum[blocks : 2 * blocks].reshape(local_rows, channels)
    high_part = returned_sum[2 * blocks :].reshape(local_rows, channels)
    from_next = passed_along(low_part, ("space", "sub"), -1)
    from_prev = passed_along(high_part, ("space", "sub"), 1)
    grad_features = (middle + from_next + from_prev).astype(jnp.bfloat16)
    output = out_sum.reshape(local_rows, channels).astype(jnp.bfloat16)
    return (output, grad_features, grand_total)


def solution(mesh):
    placed = (
        P(("space", "sub"), None),
        P(),
        P(("space", "sub"), None),
        P(("space", "sub")),
        P(("space", "sub")),
        P(("space", "sub")),
        P(("space", "sub"), None),
        P(("space", "sub")),
    )
    return jax.shard_map(
        on_device,
        mesh=mesh,
        in_specs=placed,
        out_specs=(P(("space", "sub"), None), P(("space", "sub"), None), P()),
        check_vma=False,
    )
```

```python
import functools
import math

import jax
import jax.numpy as jnp
from jax import lax
from jax.experimental import pallas as pl
from jax.experimental.pallas import tpu as pltpu
from jax.sharding import PartitionSpec as P

BLK = 128


def passed_along(value, axis, steps):
    count = lax.axis_size(axis)
    leading, last = (max(0, -steps), min(count, count - steps))
    return lax.ppermute(value, axis, [(source, source + steps) for source in range(leading, last)])


def summed_everywhere(value, axis, work, state, last_work):
    count = lax.axis_size(axis)
    me = lax.axis_index(axis)
    flat = value.reshape(-1)
    bits = count.bit_length() - 1
    split = max(bits - 2, 0)
    masks = [1 << step for step in range(split)]
    group = [0]
    for step in range(split, bits):
        group = group + [member | (1 << step) for member in group]

    def tied(flat, state, step):
        state = work(step, state)
        if step <= last_work:
            return lax.optimization_barrier((flat, state))
        return flat, state

    step = 0
    for mask in masks:
        half = flat.shape[0] // 2
        upper = (me & mask) != 0
        send = jnp.where(upper, flat[:half], flat[half:])
        keep = jnp.where(upper, flat[half:], flat[:half])
        received = lax.ppermute(send, axis, [(i, i ^ mask) for i in range(count)])
        flat, state = tied(keep + received, state, step)
        step += 1
    others = [lax.ppermute(flat, axis, [(i, i ^ mask) for i in range(count)]) for mask in group[1:]]
    for other in others:
        flat = flat + other
    flat, state = tied(flat, state, step)
    step += 1
    for mask in reversed(masks):
        upper = (me & mask) != 0
        other = lax.ppermute(flat, axis, [(i, i ^ mask) for i in range(count)])
        flat = jnp.where(upper, jnp.concatenate([other, flat]), jnp.concatenate([flat, other]))
        flat, state = tied(flat, state, step)
        step += 1
    return flat.reshape(value.shape), state


def grouped(array_in, group_size):
    return array_in.reshape((array_in.shape[0] // group_size, group_size) + array_in.shape[1:])


def picker(index, count, dtype):
    return (index[:, None] == jnp.arange(count, dtype=jnp.int32)[None, :]).astype(dtype)


def permuter(row_map, usable, dtype):
    columns = jnp.arange(row_map.shape[1], dtype=jnp.int32)
    return ((row_map[..., None] == columns[None, None, :]) & usable[..., None]).astype(dtype)


def grad_kernel(offsets, blocks_at, targets, live, window_ref, cot_ref, rows_ref, grad_ref,
                gathered_ref):
    grad_ref[...] = jnp.zeros(grad_ref.shape, grad_ref.dtype)
    source_rows = lax.broadcasted_iota(jnp.int32, (BLK, BLK), 0)

    def advance(p, carry):
        kernel_at = offsets[p]
        picks = ((rows_ref[p] == source_rows) & (p < live[0])).astype(jnp.bfloat16)
        gathered_t = jnp.dot(
            window_ref[blocks_at[p]], picks, preferred_element_type=jnp.float32
        ).astype(jnp.bfloat16)
        gathered_ref[p] = gathered_t
        grad_ref[kernel_at] += jnp.dot(
            gathered_t, cot_ref[targets[p]], preferred_element_type=jnp.float32
        )
        return carry

    lax.fori_loop(0, rows_ref.shape[0], advance, 0, unroll=UNROLL)


def sweep_kernel(first, offsets, blocks_at, targets, live, weights_t_ref, cot_ref, rows_ref,
                 gathered_ref, out_in, ret_in, out_ref, ret_ref):
    out_ref[...] = out_in[...]
    ret_ref[...] = ret_in[...]
    source_rows = lax.broadcasted_iota(jnp.int32, (BLK, BLK), 0)

    def advance(p, carry):
        pair = first + p
        kernel_at = offsets[pair]
        target_at = targets[pair]
        picks = ((rows_ref[p] == source_rows) & (pair < live[0])).astype(jnp.bfloat16)
        moved = jnp.dot(
            picks, cot_ref[target_at], preferred_element_type=jnp.float32
        ).astype(jnp.bfloat16)
        out_ref[target_at] += jnp.dot(
            weights_t_ref[kernel_at], gathered_ref[p], preferred_element_type=jnp.float32
        )
        ret_ref[blocks_at[pair]] += jnp.dot(
            moved, weights_t_ref[kernel_at], preferred_element_type=jnp.float32
        )
        return carry

    lax.fori_loop(0, rows_ref.shape[0], advance, 0, unroll=UNROLL)


UNROLL = 4
CHUNKS = 8
FIRST_STEP = 1


def rulebook_scalars(rulebook, myself, blocks, kernel_count):
    g_off_all, source_all, target_all, row_map_all, live_count = rulebook
    pair_slots = g_off_all.shape[0]
    relative = source_all // blocks - myself
    window_block = jnp.clip((relative + 1) * blocks + source_all % blocks, 0, 3 * blocks - 1)
    offsets = jnp.clip(g_off_all, 0, kernel_count - 1)
    targets = jnp.clip(target_all, 0, blocks - 1)
    live = jnp.clip(live_count, 0, pair_slots)
    return offsets, window_block, targets, live, row_map_all.reshape(pair_slots, 1, BLK)


def grad_sweep(window, grad_blocks, scalars, kernel_count):
    channels = window.shape[1]
    rows = scalars[-1]
    window_t = window.reshape(-1, BLK, channels).transpose(0, 2, 1)
    smem = pl.BlockSpec(memory_space=pltpu.SMEM)
    vmem = pl.BlockSpec(memory_space=pltpu.VMEM)
    return pl.pallas_call(
        grad_kernel,
        out_shape=(
            jax.ShapeDtypeStruct((kernel_count, channels, channels), jnp.float32),
            jax.ShapeDtypeStruct((rows.shape[0], channels, BLK), jnp.bfloat16),
        ),
        in_specs=[smem, smem, smem, smem, vmem, vmem, vmem],
        out_specs=(vmem, vmem),
    )(*scalars[:4], window_t, grad_blocks, rows)


def forward_chunk(weights_t, grad_blocks, scalars, gathered, sums, chunk, chunk_size):
    out_sum, returned_sum = sums
    smem = pl.BlockSpec(memory_space=pltpu.SMEM)

    def whole(array):
        return pl.BlockSpec(array.shape, lambda i: (0,) * array.ndim)

    def part(array):
        return pl.BlockSpec((chunk_size,) + array.shape[1:], lambda i: (chunk,) + (0,) * (array.ndim - 1))

    rows = scalars[4]
    return pl.pallas_call(
        functools.partial(sweep_kernel, chunk * chunk_size),
        grid=(1,),
        out_shape=(
            jax.ShapeDtypeStruct(out_sum.shape, jnp.float32),
            jax.ShapeDtypeStruct(returned_sum.shape, jnp.float32),
        ),
        in_specs=[smem, smem, smem, smem, whole(weights_t), whole(grad_blocks), part(rows),
                  part(gathered), whole(out_sum), whole(returned_sum)],
        out_specs=(whole(out_sum), whole(returned_sum)),
        input_output_aliases={8: 0, 9: 1},
    )(*scalars[:4], weights_t, grad_blocks, rows, gathered, out_sum, returned_sum)


def on_device(
    features, weights, cotangent, pair_offset, pair_source, pair_target, pair_rows, pair_count
):
    axis_count = lax.axis_size(("space", "sub"))
    myself = lax.axis_index(("space", "sub"))
    local_rows = features.shape[0]
    blocks = local_rows // BLK
    channels = features.shape[1]
    before = passed_along(features, ("space", "sub"), 1)
    next_side = passed_along(features, ("space", "sub"), -1)
    window = jnp.concatenate([before, features, next_side], axis=0)
    grad_blocks = cotangent.reshape(blocks, BLK, channels)
    rulebook = (pair_offset, pair_source, pair_target, pair_rows, pair_count)
    kernel_count = weights.shape[0]
    scalars = rulebook_scalars(rulebook, myself, blocks, kernel_count)
    grad_sum, gathered = grad_sweep(window, grad_blocks, scalars, kernel_count)
    grad_sum = grad_sum * (1.0 / math.sqrt(axis_count * local_rows))
    weights_t = weights.transpose(0, 2, 1)
    pair_slots = pair_offset.shape[0]
    chunk_count = CHUNKS if pair_slots % CHUNKS == 0 else 1
    chunk_size = pair_slots // chunk_count
    first_step = FIRST_STEP if axis_count & (axis_count - 1) == 0 else 0

    def exchanged(sums):
        out_t, returned_sum = sums
        low_part = returned_sum[:blocks].reshape(local_rows, channels)
        middle = returned_sum[blocks : 2 * blocks].reshape(local_rows, channels)
        high_part = returned_sum[2 * blocks :].reshape(local_rows, channels)
        from_next = passed_along(low_part, ("space", "sub"), -1)
        from_prev = passed_along(high_part, ("space", "sub"), 1)
        return out_t, (middle + from_next + from_prev).astype(jnp.bfloat16)

    def work(step, sums):
        chunk = step - first_step
        if 0 <= chunk < chunk_count:
            return forward_chunk(weights_t, grad_blocks, scalars, gathered, sums, chunk, chunk_size)
        if chunk == chunk_count:
            return exchanged(sums)
        return sums

    sums = (
        jnp.zeros((blocks, channels, BLK), jnp.float32),
        jnp.zeros((3 * blocks, BLK, channels), jnp.float32),
    )
    if axis_count & (axis_count - 1) or grad_sum.size % axis_count:
        grand_total = lax.psum(grad_sum, ("space", "sub"))
        for chunk in range(chunk_count + 1):
            sums = work(chunk + first_step, sums)
    else:
        grand_total, sums = summed_everywhere(
            grad_sum, ("space", "sub"), work, sums, first_step + chunk_count
        )
    out_t, grad_features = sums
    out_sum = out_t.transpose(0, 2, 1)
    output = out_sum.reshape(local_rows, channels).astype(jnp.bfloat16)
    return (output, grad_features, grand_total)


def solution(mesh):
    placed = (
        P(("space", "sub"), None),
        P(),
        P(("space", "sub"), None),
        P(("space", "sub")),
        P(("space", "sub")),
        P(("space", "sub")),
        P(("space", "sub"), None),
        P(("space", "sub")),
    )
    return jax.shard_map(
        on_device,
        mesh=mesh,
        in_specs=placed,
        out_specs=(P(("space", "sub"), None), P(("space", "sub"), None), P()),
        check_vma=False,
    )
```

```python
import functools
import math

import jax
import jax.numpy as jnp
from jax import lax
from jax.experimental import pallas as pl
from jax.experimental.pallas import tpu as pltpu
from jax.sharding import PartitionSpec as P

BLK = 128


def passed_along(value, axis, steps):
    count = lax.axis_size(axis)
    leading, last = (max(0, -steps), min(count, count - steps))
    return lax.ppermute(value, axis, [(source, source + steps) for source in range(leading, last)])


def summed_everywhere(value, axis, work, state, last_work):
    count = lax.axis_size(axis)
    me = lax.axis_index(axis)
    flat = value.reshape(-1)
    bits = count.bit_length() - 1
    split = max(bits - 2, 0)
    masks = [1 << step for step in range(split)]
    group = [0]
    for step in range(split, bits):
        group = group + [member | (1 << step) for member in group]

    def tied(flat, state, step):
        state = work(step, state)
        if step <= last_work:
            return lax.optimization_barrier((flat, state))
        return flat, state

    step = 0
    for mask in masks:
        half = flat.shape[0] // 2
        upper = (me & mask) != 0
        send = jnp.where(upper, flat[:half], flat[half:])
        keep = jnp.where(upper, flat[half:], flat[:half])
        received = lax.ppermute(send, axis, [(i, i ^ mask) for i in range(count)])
        flat, state = tied(keep + received, state, step)
        step += 1
    others = [lax.ppermute(flat, axis, [(i, i ^ mask) for i in range(count)]) for mask in group[1:]]
    for other in others:
        flat = flat + other
    flat, state = tied(flat, state, step)
    step += 1
    for mask in reversed(masks):
        upper = (me & mask) != 0
        other = lax.ppermute(flat, axis, [(i, i ^ mask) for i in range(count)])
        flat = jnp.where(upper, jnp.concatenate([other, flat]), jnp.concatenate([flat, other]))
        flat, state = tied(flat, state, step)
        step += 1
    return flat.reshape(value.shape), state


def grouped(array_in, group_size):
    return array_in.reshape((array_in.shape[0] // group_size, group_size) + array_in.shape[1:])


def picker(index, count, dtype):
    return (index[:, None] == jnp.arange(count, dtype=jnp.int32)[None, :]).astype(dtype)


def permuter(row_map, usable, dtype):
    columns = jnp.arange(row_map.shape[1], dtype=jnp.int32)
    return ((row_map[..., None] == columns[None, None, :]) & usable[..., None]).astype(dtype)


def grad_kernel(offsets, blocks_at, targets, live, window_ref, cot_ref, rows_ref, grad_ref,
                gathered_ref):
    grad_ref[...] = jnp.zeros(grad_ref.shape, grad_ref.dtype)
    source_rows = lax.broadcasted_iota(jnp.int32, (BLK, BLK), 0)

    def advance(p, carry):
        kernel_at = offsets[p]
        picks = ((rows_ref[p] == source_rows) & (p < live[0])).astype(jnp.bfloat16)
        gathered_t = jnp.dot(
            window_ref[blocks_at[p]], picks, preferred_element_type=jnp.float32
        ).astype(jnp.bfloat16)
        gathered_ref[p] = gathered_t
        grad_ref[kernel_at] += jnp.dot(
            gathered_t, cot_ref[targets[p]], preferred_element_type=jnp.float32
        )
        return carry

    lax.fori_loop(0, rows_ref.shape[0], advance, 0, unroll=UNROLL)


def sweep_kernel(first, offsets, blocks_at, targets, live, weights_t_ref, cot_ref, rows_ref,
                 gathered_ref, *sums):
    if len(sums) == 4:
        out_in, ret_in, out_ref, ret_ref = sums
        out_ref[...] = out_in[...]
        ret_ref[...] = ret_in[...]
    else:
        out_ref, ret_ref = sums
        out_ref[...] = jnp.zeros(out_ref.shape, out_ref.dtype)
        ret_ref[...] = jnp.zeros(ret_ref.shape, ret_ref.dtype)
    source_rows = lax.broadcasted_iota(jnp.int32, (BLK, BLK), 0)

    def advance(p, carry):
        pair = first + p
        kernel_at = offsets[pair]
        target_at = targets[pair]
        picks = ((rows_ref[p] == source_rows) & (pair < live[0])).astype(jnp.bfloat16)
        moved = jnp.dot(
            picks, cot_ref[target_at], preferred_element_type=jnp.float32
        ).astype(jnp.bfloat16)
        out_ref[target_at] += jnp.dot(
            weights_t_ref[kernel_at], gathered_ref[p], preferred_element_type=jnp.float32
        )
        ret_ref[blocks_at[pair]] += jnp.dot(
            moved, weights_t_ref[kernel_at], preferred_element_type=jnp.float32
        )
        return carry

    lax.fori_loop(0, rows_ref.shape[0], advance, 0, unroll=UNROLL)


UNROLL = 4
CHUNKS = 8
FIRST_STEP = 1


def rulebook_scalars(rulebook, myself, blocks, kernel_count):
    g_off_all, source_all, target_all, row_map_all, live_count = rulebook
    pair_slots = g_off_all.shape[0]
    relative = source_all // blocks - myself
    window_block = jnp.clip((relative + 1) * blocks + source_all % blocks, 0, 3 * blocks - 1)
    offsets = jnp.clip(g_off_all, 0, kernel_count - 1)
    targets = jnp.clip(target_all, 0, blocks - 1)
    live = jnp.clip(live_count, 0, pair_slots)
    return offsets, window_block, targets, live, row_map_all.reshape(pair_slots, 1, BLK)


def grad_sweep(window, grad_blocks, scalars, kernel_count):
    channels = window.shape[1]
    rows = scalars[-1]
    window_t = window.reshape(-1, BLK, channels).transpose(0, 2, 1)
    smem = pl.BlockSpec(memory_space=pltpu.SMEM)
    vmem = pl.BlockSpec(memory_space=pltpu.VMEM)
    return pl.pallas_call(
        grad_kernel,
        out_shape=(
            jax.ShapeDtypeStruct((kernel_count, channels, channels), jnp.float32),
            jax.ShapeDtypeStruct((rows.shape[0], channels, BLK), jnp.bfloat16),
        ),
        in_specs=[smem, smem, smem, smem, vmem, vmem, vmem],
        out_specs=(vmem, vmem),
    )(*scalars[:4], window_t, grad_blocks, rows)


def forward_chunk(weights_t, grad_blocks, scalars, gathered, sums, chunk, chunk_size):
    out_shape, returned_shape = sum_shapes(grad_blocks, gathered, scalars)
    smem = pl.BlockSpec(memory_space=pltpu.SMEM)

    def whole(shape):
        return pl.BlockSpec(shape, lambda i: (0,) * len(shape))

    def part(array):
        return pl.BlockSpec((chunk_size,) + array.shape[1:], lambda i: (chunk,) + (0,) * (array.ndim - 1))

    rows = scalars[4]
    carried = () if sums is None else tuple(sums)
    return pl.pallas_call(
        functools.partial(sweep_kernel, chunk * chunk_size),
        grid=(1,),
        out_shape=(
            jax.ShapeDtypeStruct(out_shape, jnp.float32),
            jax.ShapeDtypeStruct(returned_shape, jnp.float32),
        ),
        in_specs=[smem, smem, smem, smem, whole(weights_t.shape), whole(grad_blocks.shape), part(rows),
                  part(gathered)] + [whole(out_shape), whole(returned_shape)][: len(carried)],
        out_specs=(whole(out_shape), whole(returned_shape)),
        input_output_aliases={8: 0, 9: 1} if carried else {},
    )(*scalars[:4], weights_t, grad_blocks, rows, gathered, *carried)


def sum_shapes(grad_blocks, gathered, scalars):
    blocks, rows_per_block, channels = grad_blocks.shape
    return (blocks, channels, rows_per_block), (3 * blocks, rows_per_block, channels)


def on_device(
    features, weights, cotangent, pair_offset, pair_source, pair_target, pair_rows, pair_count
):
    axis_count = lax.axis_size(("space", "sub"))
    myself = lax.axis_index(("space", "sub"))
    local_rows = features.shape[0]
    blocks = local_rows // BLK
    channels = features.shape[1]
    before = passed_along(features, ("space", "sub"), 1)
    next_side = passed_along(features, ("space", "sub"), -1)
    window = jnp.concatenate([before, features, next_side], axis=0)
    grad_blocks = cotangent.reshape(blocks, BLK, channels)
    rulebook = (pair_offset, pair_source, pair_target, pair_rows, pair_count)
    kernel_count = weights.shape[0]
    scalars = rulebook_scalars(rulebook, myself, blocks, kernel_count)
    grad_sum, gathered = grad_sweep(window, grad_blocks, scalars, kernel_count)
    grad_sum = grad_sum * (1.0 / math.sqrt(axis_count * local_rows))
    weights_t = weights.transpose(0, 2, 1)
    pair_slots = pair_offset.shape[0]
    chunk_count = CHUNKS if pair_slots % CHUNKS == 0 else 1
    chunk_size = pair_slots // chunk_count
    first_step = FIRST_STEP if axis_count & (axis_count - 1) == 0 else 0

    def exchanged(sums):
        out_t, returned_sum = sums
        low_part = returned_sum[:blocks].reshape(local_rows, channels)
        middle = returned_sum[blocks : 2 * blocks].reshape(local_rows, channels)
        high_part = returned_sum[2 * blocks :].reshape(local_rows, channels)
        from_next = passed_along(low_part, ("space", "sub"), -1)
        from_prev = passed_along(high_part, ("space", "sub"), 1)
        return out_t, (middle + from_next + from_prev).astype(jnp.bfloat16)

    def work(step, sums):
        chunk = step - first_step
        if 0 <= chunk < chunk_count:
            return forward_chunk(weights_t, grad_blocks, scalars, gathered, sums, chunk, chunk_size)
        if chunk == chunk_count:
            return exchanged(sums)
        return sums

    sums = None
    if axis_count & (axis_count - 1) or grad_sum.size % axis_count:
        grand_total = lax.psum(grad_sum, ("space", "sub"))
        for chunk in range(chunk_count + 1):
            sums = work(chunk + first_step, sums)
    else:
        grand_total, sums = summed_everywhere(
            grad_sum, ("space", "sub"), work, sums, first_step + chunk_count
        )
    out_t, grad_features = sums
    out_sum = out_t.transpose(0, 2, 1)
    output = out_sum.reshape(local_rows, channels).astype(jnp.bfloat16)
    return (output, grad_features, grand_total)


def solution(mesh):
    placed = (
        P(("space", "sub"), None),
        P(),
        P(("space", "sub"), None),
        P(("space", "sub")),
        P(("space", "sub")),
        P(("space", "sub")),
        P(("space", "sub"), None),
        P(("space", "sub")),
    )
    return jax.shard_map(
        on_device,
        mesh=mesh,
        in_specs=placed,
        out_specs=(P(("space", "sub"), None), P(("space", "sub"), None), P()),
        check_vma=False,
    )
```

```python
import functools
import math

import jax
import jax.numpy as jnp
from jax import lax
from jax.experimental import pallas as pl
from jax.experimental.pallas import tpu as pltpu
from jax.sharding import PartitionSpec as P

BLK = 128


def passed_along(value, axis, steps):
    count = lax.axis_size(axis)
    leading, last = (max(0, -steps), min(count, count - steps))
    return lax.ppermute(value, axis, [(source, source + steps) for source in range(leading, last)])


def summed_everywhere(value, axis, work, state, last_work):
    count = lax.axis_size(axis)
    me = lax.axis_index(axis)
    flat = value.reshape(-1)
    bits = count.bit_length() - 1
    split = max(bits - 2, 0)
    masks = [1 << step for step in range(split)]
    group = [0]
    for step in range(split, bits):
        group = group + [member | (1 << step) for member in group]

    def tied(flat, state, step):
        state = work(step, state)
        if step <= last_work:
            return lax.optimization_barrier((flat, state))
        return flat, state

    step = 0
    for mask in masks:
        half = flat.shape[0] // 2
        upper = (me & mask) != 0
        send = jnp.where(upper, flat[:half], flat[half:])
        keep = jnp.where(upper, flat[half:], flat[:half])
        received = lax.ppermute(send, axis, [(i, i ^ mask) for i in range(count)])
        flat, state = tied(keep + received, state, step)
        step += 1
    others = [lax.ppermute(flat, axis, [(i, i ^ mask) for i in range(count)]) for mask in group[1:]]
    for other in others:
        flat = flat + other
    flat, state = tied(flat, state, step)
    step += 1
    for mask in reversed(masks):
        upper = (me & mask) != 0
        other = lax.ppermute(flat, axis, [(i, i ^ mask) for i in range(count)])
        flat = jnp.where(upper, jnp.concatenate([other, flat]), jnp.concatenate([flat, other]))
        flat, state = tied(flat, state, step)
        step += 1
    return flat.reshape(value.shape), state


def grouped(array_in, group_size):
    return array_in.reshape((array_in.shape[0] // group_size, group_size) + array_in.shape[1:])


def picker(index, count, dtype):
    return (index[:, None] == jnp.arange(count, dtype=jnp.int32)[None, :]).astype(dtype)


def permuter(row_map, usable, dtype):
    columns = jnp.arange(row_map.shape[1], dtype=jnp.int32)
    return ((row_map[..., None] == columns[None, None, :]) & usable[..., None]).astype(dtype)


def grad_kernel(offsets, blocks_at, targets, live, window_ref, cot_ref, rows_ref, grad_ref,
                gathered_ref):
    grad_ref[...] = jnp.zeros(grad_ref.shape, grad_ref.dtype)
    source_rows = lax.broadcasted_iota(jnp.int32, (BLK, BLK), 0)

    def advance(p, carry):
        kernel_at = offsets[p]
        picks = ((rows_ref[p] == source_rows) & (p < live[0])).astype(jnp.bfloat16)
        gathered_t = jnp.dot(
            window_ref[blocks_at[p]], picks, preferred_element_type=jnp.float32
        ).astype(jnp.bfloat16)
        gathered_ref[p] = gathered_t
        grad_ref[kernel_at] += jnp.dot(
            gathered_t, cot_ref[targets[p]], preferred_element_type=jnp.float32
        )
        return carry

    lax.fori_loop(0, rows_ref.shape[0], advance, 0, unroll=UNROLL)


def sweep_kernel(first, offsets, blocks_at, targets, live, weights_t_ref, cot_ref, rows_ref,
                 gathered_ref, *sums):
    if len(sums) == 4:
        out_in, ret_in, out_ref, ret_ref = sums
        out_ref[...] = out_in[...]
        ret_ref[...] = ret_in[...]
    else:
        out_ref, ret_ref = sums
        out_ref[...] = jnp.zeros(out_ref.shape, out_ref.dtype)
        ret_ref[...] = jnp.zeros(ret_ref.shape, ret_ref.dtype)
    source_rows = lax.broadcasted_iota(jnp.int32, (BLK, BLK), 0)

    def advance(p, carry):
        pair = first + p
        kernel_at = offsets[pair]
        target_at = targets[pair]
        picks = ((rows_ref[p] == source_rows) & (pair < live[0])).astype(jnp.bfloat16)
        moved = jnp.dot(
            picks, cot_ref[target_at], preferred_element_type=jnp.float32
        ).astype(jnp.bfloat16)
        out_ref[target_at] += jnp.dot(
            weights_t_ref[kernel_at], gathered_ref[p], preferred_element_type=jnp.float32
        )
        ret_ref[blocks_at[pair]] += jnp.dot(
            moved, weights_t_ref[kernel_at], preferred_element_type=jnp.float32
        )
        return carry

    lax.fori_loop(0, rows_ref.shape[0], advance, 0, unroll=UNROLL)


UNROLL = 16
CHUNKS = 8
FIRST_STEP = 1


def rulebook_scalars(rulebook, myself, blocks, kernel_count):
    g_off_all, source_all, target_all, row_map_all, live_count = rulebook
    pair_slots = g_off_all.shape[0]
    relative = source_all // blocks - myself
    window_block = jnp.clip((relative + 1) * blocks + source_all % blocks, 0, 3 * blocks - 1)
    offsets = jnp.clip(g_off_all, 0, kernel_count - 1)
    targets = jnp.clip(target_all, 0, blocks - 1)
    live = jnp.clip(live_count, 0, pair_slots)
    return offsets, window_block, targets, live, row_map_all.reshape(pair_slots, 1, BLK)


def grad_sweep(window, grad_blocks, scalars, kernel_count):
    channels = window.shape[1]
    rows = scalars[-1]
    window_t = window.reshape(-1, BLK, channels).transpose(0, 2, 1)
    smem = pl.BlockSpec(memory_space=pltpu.SMEM)
    vmem = pl.BlockSpec(memory_space=pltpu.VMEM)
    return pl.pallas_call(
        grad_kernel,
        out_shape=(
            jax.ShapeDtypeStruct((kernel_count, channels, channels), jnp.float32),
            jax.ShapeDtypeStruct((rows.shape[0], channels, BLK), jnp.bfloat16),
        ),
        in_specs=[smem, smem, smem, smem, vmem, vmem, vmem],
        out_specs=(vmem, vmem),
    )(*scalars[:4], window_t, grad_blocks, rows)


def forward_chunk(weights_t, grad_blocks, scalars, gathered, sums, chunk, chunk_size):
    out_shape, returned_shape = sum_shapes(grad_blocks, gathered, scalars)
    smem = pl.BlockSpec(memory_space=pltpu.SMEM)

    def whole(shape):
        return pl.BlockSpec(shape, lambda i: (0,) * len(shape))

    def part(array):
        return pl.BlockSpec((chunk_size,) + array.shape[1:], lambda i: (chunk,) + (0,) * (array.ndim - 1))

    rows = scalars[4]
    carried = () if sums is None else tuple(sums)
    return pl.pallas_call(
        functools.partial(sweep_kernel, chunk * chunk_size),
        grid=(1,),
        out_shape=(
            jax.ShapeDtypeStruct(out_shape, jnp.float32),
            jax.ShapeDtypeStruct(returned_shape, jnp.float32),
        ),
        in_specs=[smem, smem, smem, smem, whole(weights_t.shape), whole(grad_blocks.shape), part(rows),
                  part(gathered)] + [whole(out_shape), whole(returned_shape)][: len(carried)],
        out_specs=(whole(out_shape), whole(returned_shape)),
        input_output_aliases={8: 0, 9: 1} if carried else {},
    )(*scalars[:4], weights_t, grad_blocks, rows, gathered, *carried)


def sum_shapes(grad_blocks, gathered, scalars):
    blocks, rows_per_block, channels = grad_blocks.shape
    return (blocks, channels, rows_per_block), (3 * blocks, rows_per_block, channels)


def on_device(
    features, weights, cotangent, pair_offset, pair_source, pair_target, pair_rows, pair_count
):
    axis_count = lax.axis_size(("space", "sub"))
    myself = lax.axis_index(("space", "sub"))
    local_rows = features.shape[0]
    blocks = local_rows // BLK
    channels = features.shape[1]
    before = passed_along(features, ("space", "sub"), 1)
    next_side = passed_along(features, ("space", "sub"), -1)
    window = jnp.concatenate([before, features, next_side], axis=0)
    grad_blocks = cotangent.reshape(blocks, BLK, channels)
    rulebook = (pair_offset, pair_source, pair_target, pair_rows, pair_count)
    kernel_count = weights.shape[0]
    scalars = rulebook_scalars(rulebook, myself, blocks, kernel_count)
    grad_sum, gathered = grad_sweep(window, grad_blocks, scalars, kernel_count)
    grad_sum = grad_sum * (1.0 / math.sqrt(axis_count * local_rows))
    weights_t = weights.transpose(0, 2, 1)
    pair_slots = pair_offset.shape[0]
    chunk_count = CHUNKS if pair_slots % CHUNKS == 0 else 1
    chunk_size = pair_slots // chunk_count
    first_step = FIRST_STEP if axis_count & (axis_count - 1) == 0 else 0

    def exchanged(sums):
        out_t, returned_sum = sums
        low_part = returned_sum[:blocks].reshape(local_rows, channels)
        middle = returned_sum[blocks : 2 * blocks].reshape(local_rows, channels)
        high_part = returned_sum[2 * blocks :].reshape(local_rows, channels)
        from_next = passed_along(low_part, ("space", "sub"), -1)
        from_prev = passed_along(high_part, ("space", "sub"), 1)
        return out_t, (middle + from_next + from_prev).astype(jnp.bfloat16)

    def work(step, sums):
        chunk = step - first_step
        if 0 <= chunk < chunk_count:
            return forward_chunk(weights_t, grad_blocks, scalars, gathered, sums, chunk, chunk_size)
        if chunk == chunk_count:
            return exchanged(sums)
        return sums

    sums = None
    if axis_count & (axis_count - 1) or grad_sum.size % axis_count:
        grand_total = lax.psum(grad_sum, ("space", "sub"))
        for chunk in range(chunk_count + 1):
            sums = work(chunk + first_step, sums)
    else:
        grand_total, sums = summed_everywhere(
            grad_sum, ("space", "sub"), work, sums, first_step + chunk_count
        )
    out_t, grad_features = sums
    out_sum = out_t.transpose(0, 2, 1)
    output = out_sum.reshape(local_rows, channels).astype(jnp.bfloat16)
    return (output, grad_features, grand_total)


def solution(mesh):
    placed = (
        P(("space", "sub"), None),
        P(),
        P(("space", "sub"), None),
        P(("space", "sub")),
        P(("space", "sub")),
        P(("space", "sub")),
        P(("space", "sub"), None),
        P(("space", "sub")),
    )
    return jax.shard_map(
        on_device,
        mesh=mesh,
        in_specs=placed,
        out_specs=(P(("space", "sub"), None), P(("space", "sub"), None), P()),
        check_vma=False,
    )
```

```python
import functools
import math

import jax
import jax.numpy as jnp
from jax import lax
from jax.experimental import pallas as pl
from jax.experimental.pallas import tpu as pltpu
from jax.sharding import PartitionSpec as P

BLK = 128


def passed_along(value, axis, steps):
    count = lax.axis_size(axis)
    leading, last = (max(0, -steps), min(count, count - steps))
    return lax.ppermute(value, axis, [(source, source + steps) for source in range(leading, last)])


def summed_everywhere(value, axis, work, state, last_work):
    count = lax.axis_size(axis)
    me = lax.axis_index(axis)
    flat = value.reshape(-1)
    bits = count.bit_length() - 1
    split = max(bits - 2, 0)
    masks = [1 << step for step in range(split)]
    group = [0]
    for step in range(split, bits):
        group = group + [member | (1 << step) for member in group]

    def tied(flat, state, step):
        state = work(step, state)
        if step <= last_work:
            return lax.optimization_barrier((flat, state))
        return flat, state

    step = 0
    for mask in masks:
        half = flat.shape[0] // 2
        upper = (me & mask) != 0
        send = jnp.where(upper, flat[:half], flat[half:])
        keep = jnp.where(upper, flat[half:], flat[:half])
        received = lax.ppermute(send, axis, [(i, i ^ mask) for i in range(count)])
        flat, state = tied(keep + received, state, step)
        step += 1
    others = [lax.ppermute(flat, axis, [(i, i ^ mask) for i in range(count)]) for mask in group[1:]]
    for other in others:
        flat = flat + other
    flat, state = tied(flat, state, step)
    step += 1
    for mask in reversed(masks):
        upper = (me & mask) != 0
        other = lax.ppermute(flat, axis, [(i, i ^ mask) for i in range(count)])
        flat = jnp.where(upper, jnp.concatenate([other, flat]), jnp.concatenate([flat, other]))
        flat, state = tied(flat, state, step)
        step += 1
    return flat.reshape(value.shape), state


def grouped(array_in, group_size):
    return array_in.reshape((array_in.shape[0] // group_size, group_size) + array_in.shape[1:])


def picker(index, count, dtype):
    return (index[:, None] == jnp.arange(count, dtype=jnp.int32)[None, :]).astype(dtype)


def permuter(row_map, usable, dtype):
    columns = jnp.arange(row_map.shape[1], dtype=jnp.int32)
    return ((row_map[..., None] == columns[None, None, :]) & usable[..., None]).astype(dtype)


def grad_kernel(offsets, blocks_at, targets, live, window_ref, cot_ref, rows_ref, grad_ref,
                gathered_ref):
    grad_ref[...] = jnp.zeros(grad_ref.shape, grad_ref.dtype)
    source_rows = lax.broadcasted_iota(jnp.int32, (BLK, BLK), 0)

    def advance(p, carry):
        kernel_at = offsets[p]
        picks = ((rows_ref[p] == source_rows) & (p < live[0])).astype(jnp.bfloat16)
        gathered_t = jnp.dot(
            window_ref[blocks_at[p]], picks, preferred_element_type=jnp.float32
        ).astype(jnp.bfloat16)
        gathered_ref[p] = gathered_t
        grad_ref[kernel_at] += jnp.dot(
            gathered_t, cot_ref[targets[p]], preferred_element_type=jnp.float32
        )
        return carry

    lax.fori_loop(0, rows_ref.shape[0], advance, 0, unroll=UNROLL)


def sweep_kernel(first, offsets, blocks_at, targets, live, weights_t_ref, cot_ref, rows_ref,
                 gathered_ref, *sums):
    if len(sums) == 4:
        out_in, ret_in, out_ref, ret_ref = sums
        out_ref[...] = out_in[...]
        ret_ref[...] = ret_in[...]
    else:
        out_ref, ret_ref = sums
        out_ref[...] = jnp.zeros(out_ref.shape, out_ref.dtype)
        ret_ref[...] = jnp.zeros(ret_ref.shape, ret_ref.dtype)
    source_rows = lax.broadcasted_iota(jnp.int32, (BLK, BLK), 0)

    def advance(p, carry):
        pair = first + p
        kernel_at = offsets[pair]
        target_at = targets[pair]
        picks = ((rows_ref[p] == source_rows) & (pair < live[0])).astype(jnp.bfloat16)
        moved = jnp.dot(
            picks, cot_ref[target_at], preferred_element_type=jnp.float32
        ).astype(jnp.bfloat16)
        out_ref[target_at] += jnp.dot(
            weights_t_ref[kernel_at], gathered_ref[p], preferred_element_type=jnp.float32
        )
        ret_ref[blocks_at[pair]] += jnp.dot(
            moved, weights_t_ref[kernel_at], preferred_element_type=jnp.float32
        )
        return carry

    lax.fori_loop(0, rows_ref.shape[0], advance, 0, unroll=UNROLL)


UNROLL = 32
CHUNKS = 8
FIRST_STEP = 1


def rulebook_scalars(rulebook, myself, blocks, kernel_count):
    g_off_all, source_all, target_all, row_map_all, live_count = rulebook
    pair_slots = g_off_all.shape[0]
    relative = source_all // blocks - myself
    window_block = jnp.clip((relative + 1) * blocks + source_all % blocks, 0, 3 * blocks - 1)
    offsets = jnp.clip(g_off_all, 0, kernel_count - 1)
    targets = jnp.clip(target_all, 0, blocks - 1)
    live = jnp.clip(live_count, 0, pair_slots)
    return offsets, window_block, targets, live, row_map_all.reshape(pair_slots, 1, BLK)


def grad_sweep(window, grad_blocks, scalars, kernel_count):
    channels = window.shape[1]
    rows = scalars[-1]
    window_t = window.reshape(-1, BLK, channels).transpose(0, 2, 1)
    smem = pl.BlockSpec(memory_space=pltpu.SMEM)
    vmem = pl.BlockSpec(memory_space=pltpu.VMEM)
    return pl.pallas_call(
        grad_kernel,
        out_shape=(
            jax.ShapeDtypeStruct((kernel_count, channels, channels), jnp.float32),
            jax.ShapeDtypeStruct((rows.shape[0], channels, BLK), jnp.bfloat16),
        ),
        in_specs=[smem, smem, smem, smem, vmem, vmem, vmem],
        out_specs=(vmem, vmem),
    )(*scalars[:4], window_t, grad_blocks, rows)


def forward_chunk(weights_t, grad_blocks, scalars, gathered, sums, chunk, chunk_size):
    out_shape, returned_shape = sum_shapes(grad_blocks, gathered, scalars)
    smem = pl.BlockSpec(memory_space=pltpu.SMEM)

    def whole(shape):
        return pl.BlockSpec(shape, lambda i: (0,) * len(shape))

    def part(array):
        return pl.BlockSpec((chunk_size,) + array.shape[1:], lambda i: (chunk,) + (0,) * (array.ndim - 1))

    rows = scalars[4]
    carried = () if sums is None else tuple(sums)
    return pl.pallas_call(
        functools.partial(sweep_kernel, chunk * chunk_size),
        grid=(1,),
        out_shape=(
            jax.ShapeDtypeStruct(out_shape, jnp.float32),
            jax.ShapeDtypeStruct(returned_shape, jnp.float32),
        ),
        in_specs=[smem, smem, smem, smem, whole(weights_t.shape), whole(grad_blocks.shape), part(rows),
                  part(gathered)] + [whole(out_shape), whole(returned_shape)][: len(carried)],
        out_specs=(whole(out_shape), whole(returned_shape)),
        input_output_aliases={8: 0, 9: 1} if carried else {},
    )(*scalars[:4], weights_t, grad_blocks, rows, gathered, *carried)


def sum_shapes(grad_blocks, gathered, scalars):
    blocks, rows_per_block, channels = grad_blocks.shape
    return (blocks, channels, rows_per_block), (3 * blocks, rows_per_block, channels)


def on_device(
    features, weights, cotangent, pair_offset, pair_source, pair_target, pair_rows, pair_count
):
    axis_count = lax.axis_size(("space", "sub"))
    myself = lax.axis_index(("space", "sub"))
    local_rows = features.shape[0]
    blocks = local_rows // BLK
    channels = features.shape[1]
    before = passed_along(features, ("space", "sub"), 1)
    next_side = passed_along(features, ("space", "sub"), -1)
    window = jnp.concatenate([before, features, next_side], axis=0)
    grad_blocks = cotangent.reshape(blocks, BLK, channels)
    rulebook = (pair_offset, pair_source, pair_target, pair_rows, pair_count)
    kernel_count = weights.shape[0]
    scalars = rulebook_scalars(rulebook, myself, blocks, kernel_count)
    grad_sum, gathered = grad_sweep(window, grad_blocks, scalars, kernel_count)
    grad_sum = grad_sum * (1.0 / math.sqrt(axis_count * local_rows))
    weights_t = weights.transpose(0, 2, 1)
    pair_slots = pair_offset.shape[0]
    chunk_count = CHUNKS if pair_slots % CHUNKS == 0 else 1
    chunk_size = pair_slots // chunk_count
    first_step = FIRST_STEP if axis_count & (axis_count - 1) == 0 else 0

    def exchanged(sums):
        out_t, returned_sum = sums
        low_part = returned_sum[:blocks].reshape(local_rows, channels)
        middle = returned_sum[blocks : 2 * blocks].reshape(local_rows, channels)
        high_part = returned_sum[2 * blocks :].reshape(local_rows, channels)
        from_next = passed_along(low_part, ("space", "sub"), -1)
        from_prev = passed_along(high_part, ("space", "sub"), 1)
        return out_t, (middle + from_next + from_prev).astype(jnp.bfloat16)

    def work(step, sums):
        chunk = step - first_step
        if 0 <= chunk < chunk_count:
            return forward_chunk(weights_t, grad_blocks, scalars, gathered, sums, chunk, chunk_size)
        if chunk == chunk_count:
            return exchanged(sums)
        return sums

    sums = None
    if axis_count & (axis_count - 1) or grad_sum.size % axis_count:
        grand_total = lax.psum(grad_sum, ("space", "sub"))
        for chunk in range(chunk_count + 1):
            sums = work(chunk + first_step, sums)
    else:
        grand_total, sums = summed_everywhere(
            grad_sum, ("space", "sub"), work, sums, first_step + chunk_count
        )
    out_t, grad_features = sums
    out_sum = out_t.transpose(0, 2, 1)
    output = out_sum.reshape(local_rows, channels).astype(jnp.bfloat16)
    return (output, grad_features, grand_total)


def solution(mesh):
    placed = (
        P(("space", "sub"), None),
        P(),
        P(("space", "sub"), None),
        P(("space", "sub")),
        P(("space", "sub")),
        P(("space", "sub")),
        P(("space", "sub"), None),
        P(("space", "sub")),
    )
    return jax.shard_map(
        on_device,
        mesh=mesh,
        in_specs=placed,
        out_specs=(P(("space", "sub"), None), P(("space", "sub"), None), P()),
        check_vma=False,
    )
```

```python
import functools
import math

import jax
import jax.numpy as jnp
from jax import lax
from jax.experimental import pallas as pl
from jax.experimental.pallas import tpu as pltpu
from jax.sharding import PartitionSpec as P

BLK = 128


def passed_along(value, axis, steps):
    count = lax.axis_size(axis)
    leading, last = (max(0, -steps), min(count, count - steps))
    return lax.ppermute(value, axis, [(source, source + steps) for source in range(leading, last)])


def summed_everywhere(value, axis, work, state, last_work):
    count = lax.axis_size(axis)
    me = lax.axis_index(axis)
    flat = value.reshape(-1)
    bits = count.bit_length() - 1
    split = max(bits - 2, 0)
    masks = [1 << step for step in range(split)]
    group = [0]
    for step in range(split, bits):
        group = group + [member | (1 << step) for member in group]

    def tied(flat, state, step):
        state = work(step, state)
        if step <= last_work:
            return lax.optimization_barrier((flat, state))
        return flat, state

    step = 0
    for mask in masks:
        half = flat.shape[0] // 2
        upper = (me & mask) != 0
        send = jnp.where(upper, flat[:half], flat[half:])
        keep = jnp.where(upper, flat[half:], flat[:half])
        received = lax.ppermute(send, axis, [(i, i ^ mask) for i in range(count)])
        flat, state = tied(keep + received, state, step)
        step += 1
    others = [lax.ppermute(flat, axis, [(i, i ^ mask) for i in range(count)]) for mask in group[1:]]
    for other in others:
        flat = flat + other
    flat, state = tied(flat, state, step)
    step += 1
    for mask in reversed(masks):
        upper = (me & mask) != 0
        other = lax.ppermute(flat, axis, [(i, i ^ mask) for i in range(count)])
        flat = jnp.where(upper, jnp.concatenate([other, flat]), jnp.concatenate([flat, other]))
        flat, state = tied(flat, state, step)
        step += 1
    return flat.reshape(value.shape), state


def grouped(array_in, group_size):
    return array_in.reshape((array_in.shape[0] // group_size, group_size) + array_in.shape[1:])


def picker(index, count, dtype):
    return (index[:, None] == jnp.arange(count, dtype=jnp.int32)[None, :]).astype(dtype)


def permuter(row_map, usable, dtype):
    columns = jnp.arange(row_map.shape[1], dtype=jnp.int32)
    return ((row_map[..., None] == columns[None, None, :]) & usable[..., None]).astype(dtype)


def grad_kernel(offsets, blocks_at, targets, live, window_ref, cot_ref, rows_ref, grad_ref,
                gathered_ref):
    grad_ref[...] = jnp.zeros(grad_ref.shape, grad_ref.dtype)
    source_rows = lax.broadcasted_iota(jnp.int32, (BLK, BLK), 0)

    def advance(p, carry):
        kernel_at = offsets[p]
        picks = ((rows_ref[p] == source_rows) & (p < live[0])).astype(jnp.bfloat16)
        gathered_t = jnp.dot(
            window_ref[blocks_at[p]], picks, preferred_element_type=jnp.float32
        ).astype(jnp.bfloat16)
        gathered_ref[p] = gathered_t
        grad_ref[kernel_at] += jnp.dot(
            gathered_t, cot_ref[targets[p]], preferred_element_type=jnp.float32
        )
        return carry

    lax.fori_loop(0, rows_ref.shape[0], advance, 0, unroll=UNROLL)


def sweep_kernel(first, offsets, blocks_at, targets, live, weights_t_ref, cot_ref, rows_ref,
                 gathered_ref, *sums):
    if len(sums) == 4:
        out_in, ret_in, out_ref, ret_ref = sums
        out_ref[...] = out_in[...]
        ret_ref[...] = ret_in[...]
    else:
        out_ref, ret_ref = sums
        out_ref[...] = jnp.zeros(out_ref.shape, out_ref.dtype)
        ret_ref[...] = jnp.zeros(ret_ref.shape, ret_ref.dtype)
    source_rows = lax.broadcasted_iota(jnp.int32, (BLK, BLK), 0)

    def advance(p, carry):
        pair = first + p
        kernel_at = offsets[pair]
        target_at = targets[pair]
        picks = ((rows_ref[p] == source_rows) & (pair < live[0])).astype(jnp.bfloat16)
        moved = jnp.dot(
            picks, cot_ref[target_at], preferred_element_type=jnp.float32
        ).astype(jnp.bfloat16)
        out_ref[target_at] += jnp.dot(
            weights_t_ref[kernel_at], gathered_ref[p], preferred_element_type=jnp.float32
        )
        ret_ref[blocks_at[pair]] += jnp.dot(
            moved, weights_t_ref[kernel_at], preferred_element_type=jnp.float32
        )
        return carry

    lax.fori_loop(0, rows_ref.shape[0], advance, 0, unroll=UNROLL)


UNROLL = 32
CHUNKS = 8
FIRST_STEP = 1


def rulebook_scalars(rulebook, myself, blocks, kernel_count):
    g_off_all, source_all, target_all, row_map_all, live_count = rulebook
    pair_slots = g_off_all.shape[0]
    relative = source_all // blocks - myself
    window_block = jnp.clip((relative + 1) * blocks + source_all % blocks, 0, 3 * blocks - 1)
    offsets = jnp.clip(g_off_all, 0, kernel_count - 1)
    targets = jnp.clip(target_all, 0, blocks - 1)
    live = jnp.clip(live_count, 0, pair_slots)
    return offsets, window_block, targets, live, row_map_all.reshape(pair_slots, 1, BLK)


def grad_sweep(window, grad_blocks, scalars, kernel_count):
    channels = window.shape[1]
    rows = scalars[-1]
    window_t = window.reshape(-1, BLK, channels).transpose(0, 2, 1)
    smem = pl.BlockSpec(memory_space=pltpu.SMEM)
    vmem = pl.BlockSpec(memory_space=pltpu.VMEM)
    return pl.pallas_call(
        grad_kernel,
        out_shape=(
            jax.ShapeDtypeStruct((kernel_count, channels, channels), jnp.float32),
            jax.ShapeDtypeStruct((rows.shape[0], channels, BLK), jnp.bfloat16),
        ),
        in_specs=[smem, smem, smem, smem, vmem, vmem, vmem],
        out_specs=(vmem, vmem),
    )(*scalars[:4], window_t, grad_blocks, rows)


def forward_chunk(weights_t, grad_blocks, scalars, gathered, sums, chunk, chunk_size):
    out_shape, returned_shape = sum_shapes(grad_blocks, gathered, scalars)
    smem = pl.BlockSpec(memory_space=pltpu.SMEM)

    def whole(shape):
        return pl.BlockSpec(shape, lambda i: (0,) * len(shape))

    def part(array):
        return pl.BlockSpec((chunk_size,) + array.shape[1:], lambda i: (chunk,) + (0,) * (array.ndim - 1))

    rows = scalars[4]
    carried = () if sums is None else tuple(sums)
    return pl.pallas_call(
        functools.partial(sweep_kernel, chunk * chunk_size),
        grid=(1,),
        out_shape=(
            jax.ShapeDtypeStruct(out_shape, jnp.float32),
            jax.ShapeDtypeStruct(returned_shape, jnp.float32),
        ),
        in_specs=[smem, smem, smem, smem, whole(weights_t.shape), whole(grad_blocks.shape), part(rows),
                  part(gathered)] + [whole(out_shape), whole(returned_shape)][: len(carried)],
        out_specs=(whole(out_shape), whole(returned_shape)),
        input_output_aliases={8: 0, 9: 1} if carried else {},
    )(*scalars[:4], weights_t, grad_blocks, rows, gathered, *carried)


def sum_shapes(grad_blocks, gathered, scalars):
    blocks, rows_per_block, channels = grad_blocks.shape
    return (blocks, channels, rows_per_block), (3 * blocks, rows_per_block, channels)


def on_device(
    features, weights, cotangent, pair_offset, pair_source, pair_target, pair_rows, pair_count
):
    axis_count = lax.axis_size(("space", "sub"))
    myself = lax.axis_index(("space", "sub"))
    local_rows = features.shape[0]
    blocks = local_rows // BLK
    channels = features.shape[1]
    before = passed_along(features, ("space", "sub"), 1)
    next_side = passed_along(features, ("space", "sub"), -1)
    window = jnp.concatenate([before, features, next_side], axis=0)
    grad_blocks = cotangent.reshape(blocks, BLK, channels)
    rulebook = (pair_offset, pair_source, pair_target, pair_rows, pair_count)
    kernel_count = weights.shape[0]
    scalars = rulebook_scalars(rulebook, myself, blocks, kernel_count)
    grad_sum, gathered = grad_sweep(window, grad_blocks, scalars, kernel_count)
    grad_sum = grad_sum * (1.0 / math.sqrt(axis_count * local_rows))
    pair_slots = pair_offset.shape[0]
    chunk_count = CHUNKS if pair_slots % CHUNKS == 0 else 1
    chunk_size = pair_slots // chunk_count
    power_of_two = axis_count & (axis_count - 1) == 0 and grad_sum.size % axis_count == 0
    first_step = FIRST_STEP if power_of_two else 0
    split = max(axis_count.bit_length() - 3, 0)
    exchange_step = max(first_step + chunk_count, 2 * split - 1)

    def exchanged(sums):
        out_t, returned_sum = sums
        low_part = returned_sum[:blocks].reshape(local_rows, channels)
        middle = returned_sum[blocks : 2 * blocks].reshape(local_rows, channels)
        high_part = returned_sum[2 * blocks :].reshape(local_rows, channels)
        from_next = passed_along(low_part, ("space", "sub"), -1)
        from_prev = passed_along(high_part, ("space", "sub"), 1)
        return out_t, (middle + from_next + from_prev).astype(jnp.bfloat16)

    def work(step, state):
        weights_t, sums = state
        if weights_t is None:
            weights_t = weights.transpose(0, 2, 1)
        chunk = step - first_step
        if 0 <= chunk < chunk_count:
            sums = forward_chunk(weights_t, grad_blocks, scalars, gathered, sums, chunk, chunk_size)
        elif step == exchange_step:
            sums = exchanged(sums)
        return weights_t, sums

    state = (None, None)
    if power_of_two:
        grand_total, state = summed_everywhere(
            grad_sum, ("space", "sub"), work, state, exchange_step
        )
    else:
        grand_total = lax.psum(grad_sum, ("space", "sub"))
        for step in range(exchange_step + 1):
            state = work(step, state)
    out_t, grad_features = state[1]
    out_sum = out_t.transpose(0, 2, 1)
    output = out_sum.reshape(local_rows, channels).astype(jnp.bfloat16)
    return (output, grad_features, grand_total)


def solution(mesh):
    placed = (
        P(("space", "sub"), None),
        P(),
        P(("space", "sub"), None),
        P(("space", "sub")),
        P(("space", "sub")),
        P(("space", "sub")),
        P(("space", "sub"), None),
        P(("space", "sub")),
    )
    return jax.shard_map(
        on_device,
        mesh=mesh,
        in_specs=placed,
        out_specs=(P(("space", "sub"), None), P(("space", "sub"), None), P()),
        check_vma=False,
    )
```

```python
import functools
import math

import jax
import jax.numpy as jnp
from jax import lax
from jax.experimental import pallas as pl
from jax.experimental.pallas import tpu as pltpu
from jax.sharding import PartitionSpec as P

BLK = 128


def passed_along(value, axis, steps):
    count = lax.axis_size(axis)
    leading, last = (max(0, -steps), min(count, count - steps))
    return lax.ppermute(value, axis, [(source, source + steps) for source in range(leading, last)])


def summed_everywhere(value, axis, work, state, last_work):
    count = lax.axis_size(axis)
    me = lax.axis_index(axis)
    flat = value.reshape(-1)
    bits = count.bit_length() - 1
    split = max(bits - 2, 0)
    masks = [1 << step for step in range(split)]
    group = [0]
    for step in range(split, bits):
        group = group + [member | (1 << step) for member in group]

    def tied(flat, state, step):
        state = work(step, state)
        if step <= last_work:
            return lax.optimization_barrier((flat, state))
        return flat, state

    step = 0
    for mask in masks:
        half = flat.shape[0] // 2
        upper = (me & mask) != 0
        send = jnp.where(upper, flat[:half], flat[half:])
        keep = jnp.where(upper, flat[half:], flat[:half])
        received = lax.ppermute(send, axis, [(i, i ^ mask) for i in range(count)])
        flat, state = tied(keep + received, state, step)
        step += 1
    others = [lax.ppermute(flat, axis, [(i, i ^ mask) for i in range(count)]) for mask in group[1:]]
    for other in others:
        flat = flat + other
    flat, state = tied(flat, state, step)
    step += 1
    for mask in reversed(masks):
        upper = (me & mask) != 0
        other = lax.ppermute(flat, axis, [(i, i ^ mask) for i in range(count)])
        flat = jnp.where(upper, jnp.concatenate([other, flat]), jnp.concatenate([flat, other]))
        flat, state = tied(flat, state, step)
        step += 1
    return flat.reshape(value.shape), state


def grouped(array_in, group_size):
    return array_in.reshape((array_in.shape[0] // group_size, group_size) + array_in.shape[1:])


def picker(index, count, dtype):
    return (index[:, None] == jnp.arange(count, dtype=jnp.int32)[None, :]).astype(dtype)


def permuter(row_map, usable, dtype):
    columns = jnp.arange(row_map.shape[1], dtype=jnp.int32)
    return ((row_map[..., None] == columns[None, None, :]) & usable[..., None]).astype(dtype)


def grad_kernel(offsets, blocks_at, targets, live, window_ref, cot_ref, rows_ref, grad_ref,
                gathered_ref):
    grad_ref[...] = jnp.zeros(grad_ref.shape, grad_ref.dtype)
    source_rows = lax.broadcasted_iota(jnp.int32, (BLK, BLK), 0)

    def advance(p, carry):
        kernel_at = offsets[p]
        picks = ((rows_ref[p] == source_rows) & (p < live[0])).astype(jnp.bfloat16)
        gathered_t = jnp.dot(
            window_ref[blocks_at[p]], picks, preferred_element_type=jnp.float32
        ).astype(jnp.bfloat16)
        gathered_ref[p] = gathered_t
        grad_ref[kernel_at] += jnp.dot(
            gathered_t, cot_ref[targets[p]], preferred_element_type=jnp.float32
        )
        return carry

    lax.fori_loop(0, rows_ref.shape[0], advance, 0, unroll=UNROLL)


def sweep_kernel(first, offsets, blocks_at, targets, live, weights_t_ref, cot_ref, rows_ref,
                 gathered_ref, *sums):
    if len(sums) == 4:
        out_in, ret_in, out_ref, ret_ref = sums
        out_ref[...] = out_in[...]
        ret_ref[...] = ret_in[...]
    else:
        out_ref, ret_ref = sums
        out_ref[...] = jnp.zeros(out_ref.shape, out_ref.dtype)
        ret_ref[...] = jnp.zeros(ret_ref.shape, ret_ref.dtype)
    source_rows = lax.broadcasted_iota(jnp.int32, (BLK, BLK), 0)

    def advance(p, carry):
        pair = first + p
        kernel_at = offsets[pair]
        target_at = targets[pair]
        picks = ((rows_ref[p] == source_rows) & (pair < live[0])).astype(jnp.bfloat16)
        moved = jnp.dot(
            picks, cot_ref[target_at], preferred_element_type=jnp.float32
        ).astype(jnp.bfloat16)
        out_ref[target_at] += jnp.dot(
            weights_t_ref[kernel_at], gathered_ref[p], preferred_element_type=jnp.float32
        )
        ret_ref[blocks_at[pair]] += jnp.dot(
            moved, weights_t_ref[kernel_at], preferred_element_type=jnp.float32
        )
        return carry

    lax.fori_loop(0, rows_ref.shape[0], advance, 0, unroll=UNROLL)


UNROLL = 32
CHUNKS = 8
FIRST_STEP = 0


def rulebook_scalars(rulebook, myself, blocks, kernel_count):
    g_off_all, source_all, target_all, row_map_all, live_count = rulebook
    pair_slots = g_off_all.shape[0]
    relative = source_all // blocks - myself
    window_block = jnp.clip((relative + 1) * blocks + source_all % blocks, 0, 3 * blocks - 1)
    offsets = jnp.clip(g_off_all, 0, kernel_count - 1)
    targets = jnp.clip(target_all, 0, blocks - 1)
    live = jnp.clip(live_count, 0, pair_slots)
    return offsets, window_block, targets, live, row_map_all.reshape(pair_slots, 1, BLK)


def grad_sweep(window, grad_blocks, scalars, kernel_count):
    channels = window.shape[1]
    rows = scalars[-1]
    window_t = window.reshape(-1, BLK, channels).transpose(0, 2, 1)
    smem = pl.BlockSpec(memory_space=pltpu.SMEM)
    vmem = pl.BlockSpec(memory_space=pltpu.VMEM)
    return pl.pallas_call(
        grad_kernel,
        out_shape=(
            jax.ShapeDtypeStruct((kernel_count, channels, channels), jnp.float32),
            jax.ShapeDtypeStruct((rows.shape[0], channels, BLK), jnp.bfloat16),
        ),
        in_specs=[smem, smem, smem, smem, vmem, vmem, vmem],
        out_specs=(vmem, vmem),
    )(*scalars[:4], window_t, grad_blocks, rows)


def forward_chunk(weights_t, grad_blocks, scalars, gathered, sums, chunk, chunk_size):
    out_shape, returned_shape = sum_shapes(grad_blocks, gathered, scalars)
    smem = pl.BlockSpec(memory_space=pltpu.SMEM)

    def whole(shape):
        return pl.BlockSpec(shape, lambda i: (0,) * len(shape))

    def part(array):
        return pl.BlockSpec((chunk_size,) + array.shape[1:], lambda i: (chunk,) + (0,) * (array.ndim - 1))

    rows = scalars[4]
    carried = () if sums is None else tuple(sums)
    return pl.pallas_call(
        functools.partial(sweep_kernel, chunk * chunk_size),
        grid=(1,),
        out_shape=(
            jax.ShapeDtypeStruct(out_shape, jnp.float32),
            jax.ShapeDtypeStruct(returned_shape, jnp.float32),
        ),
        in_specs=[smem, smem, smem, smem, whole(weights_t.shape), whole(grad_blocks.shape), part(rows),
                  part(gathered)] + [whole(out_shape), whole(returned_shape)][: len(carried)],
        out_specs=(whole(out_shape), whole(returned_shape)),
        input_output_aliases={8: 0, 9: 1} if carried else {},
    )(*scalars[:4], weights_t, grad_blocks, rows, gathered, *carried)


def sum_shapes(grad_blocks, gathered, scalars):
    blocks, rows_per_block, channels = grad_blocks.shape
    return (blocks, channels, rows_per_block), (3 * blocks, rows_per_block, channels)


def on_device(
    features, weights, cotangent, pair_offset, pair_source, pair_target, pair_rows, pair_count
):
    axis_count = lax.axis_size(("space", "sub"))
    myself = lax.axis_index(("space", "sub"))
    local_rows = features.shape[0]
    blocks = local_rows // BLK
    channels = features.shape[1]
    before = passed_along(features, ("space", "sub"), 1)
    next_side = passed_along(features, ("space", "sub"), -1)
    window = jnp.concatenate([before, features, next_side], axis=0)
    grad_blocks = cotangent.reshape(blocks, BLK, channels)
    rulebook = (pair_offset, pair_source, pair_target, pair_rows, pair_count)
    kernel_count = weights.shape[0]
    scalars = rulebook_scalars(rulebook, myself, blocks, kernel_count)
    grad_sum, gathered = grad_sweep(window, grad_blocks, scalars, kernel_count)
    grad_sum = grad_sum * (1.0 / math.sqrt(axis_count * local_rows))
    pair_slots = pair_offset.shape[0]
    chunk_count = CHUNKS if pair_slots % CHUNKS == 0 else 1
    chunk_size = pair_slots // chunk_count
    power_of_two = axis_count & (axis_count - 1) == 0 and grad_sum.size % axis_count == 0
    first_step = FIRST_STEP if power_of_two else 0
    split = max(axis_count.bit_length() - 3, 0)
    exchange_step = max(first_step + chunk_count, 2 * split - 1)

    def exchanged(sums):
        out_t, returned_sum = sums
        low_part = returned_sum[:blocks].reshape(local_rows, channels)
        middle = returned_sum[blocks : 2 * blocks].reshape(local_rows, channels)
        high_part = returned_sum[2 * blocks :].reshape(local_rows, channels)
        from_next = passed_along(low_part, ("space", "sub"), -1)
        from_prev = passed_along(high_part, ("space", "sub"), 1)
        return out_t, (middle + from_next + from_prev).astype(jnp.bfloat16)

    def work(step, state):
        weights_t, sums = state
        if weights_t is None:
            weights_t = weights.transpose(0, 2, 1)
        chunk = step - first_step
        if 0 <= chunk < chunk_count:
            sums = forward_chunk(weights_t, grad_blocks, scalars, gathered, sums, chunk, chunk_size)
        elif step == exchange_step:
            sums = exchanged(sums)
        return weights_t, sums

    state = (None, None)
    if power_of_two:
        grand_total, state = summed_everywhere(
            grad_sum, ("space", "sub"), work, state, exchange_step
        )
    else:
        grand_total = lax.psum(grad_sum, ("space", "sub"))
        for step in range(exchange_step + 1):
            state = work(step, state)
    out_t, grad_features = state[1]
    out_sum = out_t.transpose(0, 2, 1)
    output = out_sum.reshape(local_rows, channels).astype(jnp.bfloat16)
    return (output, grad_features, grand_total)


def solution(mesh):
    placed = (
        P(("space", "sub"), None),
        P(),
        P(("space", "sub"), None),
        P(("space", "sub")),
        P(("space", "sub")),
        P(("space", "sub")),
        P(("space", "sub"), None),
        P(("space", "sub")),
    )
    return jax.shard_map(
        on_device,
        mesh=mesh,
        in_specs=placed,
        out_specs=(P(("space", "sub"), None), P(("space", "sub"), None), P()),
        check_vma=False,
    )
```

```python
import functools
import math

import jax
import jax.numpy as jnp
from jax import lax
from jax.experimental import pallas as pl
from jax.experimental.pallas import tpu as pltpu
from jax.sharding import PartitionSpec as P

BLK = 128


def passed_along(value, axis, steps):
    count = lax.axis_size(axis)
    leading, last = (max(0, -steps), min(count, count - steps))
    return lax.ppermute(value, axis, [(source, source + steps) for source in range(leading, last)])


def summed_everywhere(value, axis, work, state, last_work):
    count = lax.axis_size(axis)
    me = lax.axis_index(axis)
    flat = value.reshape(-1)
    bits = count.bit_length() - 1
    split = max(bits - 2, 0)
    masks = [1 << step for step in range(split)]
    group = [0]
    for step in range(split, bits):
        group = group + [member | (1 << step) for member in group]

    def tied(flat, state, step):
        state = work(step, state)
        if step <= last_work:
            return lax.optimization_barrier((flat, state))
        return flat, state

    step = 0
    for mask in masks:
        half = flat.shape[0] // 2
        upper = (me & mask) != 0
        send = jnp.where(upper, flat[:half], flat[half:])
        keep = jnp.where(upper, flat[half:], flat[:half])
        received = lax.ppermute(send, axis, [(i, i ^ mask) for i in range(count)])
        flat, state = tied(keep + received, state, step)
        step += 1
    others = [lax.ppermute(flat, axis, [(i, i ^ mask) for i in range(count)]) for mask in group[1:]]
    for other in others:
        flat = flat + other
    flat, state = tied(flat, state, step)
    step += 1
    for mask in reversed(masks):
        upper = (me & mask) != 0
        other = lax.ppermute(flat, axis, [(i, i ^ mask) for i in range(count)])
        flat = jnp.where(upper, jnp.concatenate([other, flat]), jnp.concatenate([flat, other]))
        flat, state = tied(flat, state, step)
        step += 1
    return flat.reshape(value.shape), state


def grouped(array_in, group_size):
    return array_in.reshape((array_in.shape[0] // group_size, group_size) + array_in.shape[1:])


def picker(index, count, dtype):
    return (index[:, None] == jnp.arange(count, dtype=jnp.int32)[None, :]).astype(dtype)


def permuter(row_map, usable, dtype):
    columns = jnp.arange(row_map.shape[1], dtype=jnp.int32)
    return ((row_map[..., None] == columns[None, None, :]) & usable[..., None]).astype(dtype)


def grad_kernel(offsets, blocks_at, targets, live, window_ref, cot_ref, rows_ref, grad_ref,
                gathered_ref):
    grad_ref[...] = jnp.zeros(grad_ref.shape, grad_ref.dtype)
    source_rows = lax.broadcasted_iota(jnp.int32, (BLK, BLK), 0)

    def advance(p, carry):
        kernel_at = offsets[p]
        picks = ((rows_ref[p] == source_rows) & (p < live[0])).astype(jnp.bfloat16)
        gathered_t = jnp.dot(
            window_ref[blocks_at[p]], picks, preferred_element_type=jnp.float32
        ).astype(jnp.bfloat16)
        gathered_ref[p] = gathered_t
        grad_ref[kernel_at] += jnp.dot(
            gathered_t, cot_ref[targets[p]], preferred_element_type=jnp.float32
        )
        return carry

    lax.fori_loop(0, rows_ref.shape[0], advance, 0, unroll=min(UNROLL, rows_ref.shape[0]))


def sweep_kernel(first, offsets, blocks_at, targets, live, weights_t_ref, cot_ref, rows_ref,
                 gathered_ref, *sums):
    if len(sums) == 4:
        out_in, ret_in, out_ref, ret_ref = sums
        out_ref[...] = out_in[...]
        ret_ref[...] = ret_in[...]
    else:
        out_ref, ret_ref = sums
        out_ref[...] = jnp.zeros(out_ref.shape, out_ref.dtype)
        ret_ref[...] = jnp.zeros(ret_ref.shape, ret_ref.dtype)
    source_rows = lax.broadcasted_iota(jnp.int32, (BLK, BLK), 0)

    def advance(p, carry):
        pair = first + p
        kernel_at = offsets[pair]
        target_at = targets[pair]
        picks = ((rows_ref[p] == source_rows) & (pair < live[0])).astype(jnp.bfloat16)
        moved = jnp.dot(
            picks, cot_ref[target_at], preferred_element_type=jnp.float32
        ).astype(jnp.bfloat16)
        out_ref[target_at] += jnp.dot(
            weights_t_ref[kernel_at], gathered_ref[p], preferred_element_type=jnp.float32
        )
        ret_ref[blocks_at[pair]] += jnp.dot(
            moved, weights_t_ref[kernel_at], preferred_element_type=jnp.float32
        )
        return carry

    lax.fori_loop(0, rows_ref.shape[0], advance, 0, unroll=min(UNROLL, rows_ref.shape[0]))


UNROLL = 64
CHUNKS = 8
FIRST_STEP = 0


def rulebook_scalars(rulebook, myself, blocks, kernel_count):
    g_off_all, source_all, target_all, row_map_all, live_count = rulebook
    pair_slots = g_off_all.shape[0]
    relative = source_all // blocks - myself
    window_block = jnp.clip((relative + 1) * blocks + source_all % blocks, 0, 3 * blocks - 1)
    offsets = jnp.clip(g_off_all, 0, kernel_count - 1)
    targets = jnp.clip(target_all, 0, blocks - 1)
    live = jnp.clip(live_count, 0, pair_slots)
    return offsets, window_block, targets, live, row_map_all.reshape(pair_slots, 1, BLK)


def grad_sweep(window, grad_blocks, scalars, kernel_count):
    channels = window.shape[1]
    rows = scalars[-1]
    window_t = window.reshape(-1, BLK, channels).transpose(0, 2, 1)
    smem = pl.BlockSpec(memory_space=pltpu.SMEM)
    vmem = pl.BlockSpec(memory_space=pltpu.VMEM)
    return pl.pallas_call(
        grad_kernel,
        out_shape=(
            jax.ShapeDtypeStruct((kernel_count, channels, channels), jnp.float32),
            jax.ShapeDtypeStruct((rows.shape[0], channels, BLK), jnp.bfloat16),
        ),
        in_specs=[smem, smem, smem, smem, vmem, vmem, vmem],
        out_specs=(vmem, vmem),
    )(*scalars[:4], window_t, grad_blocks, rows)


def forward_chunk(weights_t, grad_blocks, scalars, gathered, sums, chunk, chunk_size):
    out_shape, returned_shape = sum_shapes(grad_blocks, gathered, scalars)
    smem = pl.BlockSpec(memory_space=pltpu.SMEM)

    def whole(shape):
        return pl.BlockSpec(shape, lambda i: (0,) * len(shape))

    def part(array):
        return pl.BlockSpec((chunk_size,) + array.shape[1:], lambda i: (chunk,) + (0,) * (array.ndim - 1))

    rows = scalars[4]
    carried = () if sums is None else tuple(sums)
    return pl.pallas_call(
        functools.partial(sweep_kernel, chunk * chunk_size),
        grid=(1,),
        out_shape=(
            jax.ShapeDtypeStruct(out_shape, jnp.float32),
            jax.ShapeDtypeStruct(returned_shape, jnp.float32),
        ),
        in_specs=[smem, smem, smem, smem, whole(weights_t.shape), whole(grad_blocks.shape), part(rows),
                  part(gathered)] + [whole(out_shape), whole(returned_shape)][: len(carried)],
        out_specs=(whole(out_shape), whole(returned_shape)),
        input_output_aliases={8: 0, 9: 1} if carried else {},
    )(*scalars[:4], weights_t, grad_blocks, rows, gathered, *carried)


def sum_shapes(grad_blocks, gathered, scalars):
    blocks, rows_per_block, channels = grad_blocks.shape
    return (blocks, channels, rows_per_block), (3 * blocks, rows_per_block, channels)


def on_device(
    features, weights, cotangent, pair_offset, pair_source, pair_target, pair_rows, pair_count
):
    axis_count = lax.axis_size(("space", "sub"))
    myself = lax.axis_index(("space", "sub"))
    local_rows = features.shape[0]
    blocks = local_rows // BLK
    channels = features.shape[1]
    before = passed_along(features, ("space", "sub"), 1)
    next_side = passed_along(features, ("space", "sub"), -1)
    window = jnp.concatenate([before, features, next_side], axis=0)
    grad_blocks = cotangent.reshape(blocks, BLK, channels)
    rulebook = (pair_offset, pair_source, pair_target, pair_rows, pair_count)
    kernel_count = weights.shape[0]
    scalars = rulebook_scalars(rulebook, myself, blocks, kernel_count)
    grad_sum, gathered = grad_sweep(window, grad_blocks, scalars, kernel_count)
    grad_sum = grad_sum * (1.0 / math.sqrt(axis_count * local_rows))
    pair_slots = pair_offset.shape[0]
    chunk_count = CHUNKS if pair_slots % CHUNKS == 0 else 1
    chunk_size = pair_slots // chunk_count
    power_of_two = axis_count & (axis_count - 1) == 0 and grad_sum.size % axis_count == 0
    first_step = FIRST_STEP if power_of_two else 0
    split = max(axis_count.bit_length() - 3, 0)
    exchange_step = max(first_step + chunk_count, 2 * split - 1)

    def exchanged(sums):
        out_t, returned_sum = sums
        low_part = returned_sum[:blocks].reshape(local_rows, channels)
        middle = returned_sum[blocks : 2 * blocks].reshape(local_rows, channels)
        high_part = returned_sum[2 * blocks :].reshape(local_rows, channels)
        from_next = passed_along(low_part, ("space", "sub"), -1)
        from_prev = passed_along(high_part, ("space", "sub"), 1)
        return out_t, (middle + from_next + from_prev).astype(jnp.bfloat16)

    def work(step, state):
        weights_t, sums = state
        if weights_t is None:
            weights_t = weights.transpose(0, 2, 1)
        chunk = step - first_step
        if 0 <= chunk < chunk_count:
            sums = forward_chunk(weights_t, grad_blocks, scalars, gathered, sums, chunk, chunk_size)
        elif step == exchange_step:
            sums = exchanged(sums)
        return weights_t, sums

    state = (None, None)
    if power_of_two:
        grand_total, state = summed_everywhere(
            grad_sum, ("space", "sub"), work, state, exchange_step
        )
    else:
        grand_total = lax.psum(grad_sum, ("space", "sub"))
        for step in range(exchange_step + 1):
            state = work(step, state)
    out_t, grad_features = state[1]
    out_sum = out_t.transpose(0, 2, 1)
    output = out_sum.reshape(local_rows, channels).astype(jnp.bfloat16)
    return (output, grad_features, grand_total)


def solution(mesh):
    placed = (
        P(("space", "sub"), None),
        P(),
        P(("space", "sub"), None),
        P(("space", "sub")),
        P(("space", "sub")),
        P(("space", "sub")),
        P(("space", "sub"), None),
        P(("space", "sub")),
    )
    return jax.shard_map(
        on_device,
        mesh=mesh,
        in_specs=placed,
        out_specs=(P(("space", "sub"), None), P(("space", "sub"), None), P()),
        check_vma=False,
    )
```
